1024 devices in a mesh: seq: 64 (over z, y_lo, core), chan: 16 (over x, y_hi).
Axes of the slice: x: 8, y: 8 (y_hi: 2, y_lo: 4; y = y_hi * 4 + y_lo), z: 8, core: 2. Of those that a mesh axis runs over, the one named last changes fastest.
Arguments:
- queries: bfloat16 [8192, 4096], P('seq', 'chan'), may hold values from -6 to 6
- keys: bfloat16 [8192, 4096], P('seq', 'chan'), may hold values from -6 to 6
- values: bfloat16 [8192, 4096], P('seq', 'chan'), may hold values from -6 to 6
- short_taps: float32 [3, 3, 4096], P(None, None, 'chan'), may hold values from -3 to 3
- long_filter: float32 [4096, 8192], P(('chan', 'seq')), may hold values from -1 to 1
- skip_gain: float32 [4096], P(('chan', 'seq')), may hold values from -1 to 1
- out_weight: bfloat16 [4096, 4096], P(None, 'chan'), may hold values from -0.09375 to 0.09375
Outputs:
- block_out: bfloat16 [8192, 4096], P('seq', 'chan')
The draws below stay inside these ranges and needn't reach their ends.
All inputs are finite; a program needn't handle non-finite values.
Results may differ from the reference program's by a relative error of at most 0.012.
Values may be sent and summed in bfloat16 or wider, within the bound.
No kernel may reach another device: no remote copies, remote signals or barrier semaphores. Data moves between devices by JAX's collectives and lax.ppermute only.
A program may use at most 32 MiB of HBM per device.

```python
import math
import jax
import jax.numpy as jnp
from jax import lax

D = 4096
SPAN = 3
TOKENS = 8192


def mode_amplitude(rate):
    return jnp.sqrt(2.0 * rate / (1.0 - jnp.exp(-2.0 * rate * TOKENS)))


def draw_long_filter(key, part):
    key_share, key_slow, key_fast, key_rough = jax.random.split(key, 4)
    share = jax.random.uniform(key_share, (D,), jnp.float32, 0.2, 0.8)
    slow_rate = jnp.exp(jax.random.uniform(key_slow, (D,), jnp.float32, math.log(0.2 / TOKENS), math.log(2.0 / TOKENS)))
    fast_rate = jnp.exp(jax.random.uniform(key_fast, (D,), jnp.float32, math.log(1.0 / 50.0), math.log(1.0 / 20.0)))
    position = jnp.arange(TOKENS).astype(jnp.float32)
    fast_part = (jnp.sqrt(1.0 - share) * mode_amplitude(fast_rate))[:, None] * jnp.exp(-fast_rate[:, None] * position[None, :])
    slow_part = (jnp.sqrt(share) * mode_amplitude(slow_rate))[:, None] * jnp.exp(-slow_rate[:, None] * position[None, :])
    rough = jax.random.uniform(key_rough, (D, TOKENS), jnp.float32, -1.7, 1.7)
    return jnp.clip(rough * (fast_part + slow_part), -1.0, 1.0)


def block_levels(own_key, shape, cuts, least, high):
    loudness = 1.0
    for dim, parts in cuts:
        heights = jax.random.uniform(jax.random.fold_in(jax.random.fold_in(own_key, 6), dim), (parts,), jnp.float32, least / len(cuts), high / len(cuts))
        loudness = loudness * jnp.repeat(jnp.exp(heights), shape[dim] // parts).reshape((-1,) + (1,) * (len(shape) - 1 - dim))
    return loudness


def normal_values(stream_key, shape, deviation, reach, cuts=(), held_as=jnp.bfloat16):
    factor_of = block_levels(stream_key, shape, cuts, -0.22, 0.18) if cuts else 1.0
    values = jax.random.normal(stream_key, shape, jnp.float32) * deviation * factor_of
    return jnp.minimum(jnp.maximum(values, -reach), reach).astype(held_as)


def setup_inputs(seed: int = 0) -> dict:
    key_list = jax.random.split(jax.random.key(seed), 8)
    queries = normal_values(key_list[0], (TOKENS, D), 1.0, 6.0, ((0, 64), (1, 16)))
    keys = normal_values(key_list[1], (TOKENS, D), 1.0, 6.0, ((0, 64), (1, 16)))
    values = normal_values(key_list[2], (TOKENS, D), 1.0, 6.0, ((0, 64), (1, 16)))
    short_taps = normal_values(key_list[3], (3, SPAN, D), 0.6, 3.0, ((2, 16),), jnp.float32)
    long_filter = draw_long_filter(jax.random.fold_in(key_list[7], 71), 0)
    skip_gain = jnp.clip(jax.random.uniform(key_list[5], (D,), jnp.float32, -1.0, 1.0) * block_levels(key_list[5], (D,), ((0, 1024),), -0.4, 0.0), -1.0, 1.0)
    out_weight = normal_values(key_list[6], (D, D), D ** -0.5, 0.09375, ((1, 16),))
    return dict(queries=queries, keys=keys, values=values, short_taps=short_taps, long_filter=long_filter, skip_gain=skip_gain, out_weight=out_weight)


def short_filter(features, taps):
    values_f = features.astype(jnp.float32)
    total = taps[0] * values_f
    for offset in range(1, taps.shape[0]):
        moved = jnp.concatenate([jnp.zeros((offset, values_f.shape[1]), jnp.float32), values_f[:-offset]], 0)
        total = total + taps[offset] * moved
    return total


def reference(queries, keys, values, short_taps, long_filter, skip_gain, out_weight):
    short_q = short_filter(queries, short_taps[0]).astype(jnp.bfloat16)
    mixed = (short_filter(keys, short_taps[1]) * short_filter(values, short_taps[2])).astype(jnp.bfloat16)
    width = mixed.shape[1]
    block = min(256, width)
    total = 2 * TOKENS

    def convolve(pieces):
        signal, filters, gains = pieces
        spec_signal = jnp.fft.rfft(signal, n=total, axis=1)
        spec_filter = jnp.fft.rfft(filters, n=total, axis=1)
        result = jnp.fft.irfft(spec_signal * spec_filter, n=total, axis=1)[:, :TOKENS]
        return result + gains[:, None] * signal

    signal_all = mixed.astype(jnp.float32).T.reshape(width // block, block, TOKENS)
    filter_all = long_filter.reshape(width // block, block, TOKENS)
    gain_all = skip_gain.reshape(width // block, block)
    long_out = lax.map(convolve, (signal_all, filter_all, gain_all)).reshape(width, TOKENS).T.astype(jnp.bfloat16)
    gated = (short_q.astype(jnp.float32) * long_out.astype(jnp.float32)).astype(jnp.bfloat16)
    return jnp.dot(gated, out_weight, preferred_element_type=jnp.float32).astype(jnp.bfloat16)
```

```python
import math

import jax
import jax.numpy as jnp
from jax import lax
from jax.sharding import PartitionSpec as P

HIGHEST_MODE = lax.Precision.HIGHEST


def shifted(block, axis, distance):
    devices = range(lax.axis_size(axis))
    route = [(i - distance, i) for i in devices if i - distance in devices]
    return lax.ppermute(block, axis, route)


def tables(count):
    index = jnp.arange(count, dtype=jnp.int32)
    phase = (index[:, None] * index[None, :] % count).astype(jnp.float32) * (2.0 * math.pi / count)
    return (jnp.cos(phase), jnp.sin(phase))


def twiddle(outer, inner, total):
    first = jnp.arange(outer, dtype=jnp.int32)
    second = jnp.arange(inner, dtype=jnp.int32)
    phase = (first[:, None] * second[None, :] % total).astype(jnp.float32) * (2.0 * math.pi / total)
    return (jnp.cos(phase), jnp.sin(phase))


def split_factor(length):
    total = 2 * length
    best = 1
    candidate = 1
    while candidate * candidate <= total:
        if length % candidate == 0:
            best = candidate
        candidate += 1
    return (best, total // best)


def spectrum(signal, inner, outer, outer_tables, inner_tables, turn_tables):
    cos_out, sin_out = outer_tables
    cos_in, sin_in = inner_tables
    turn_cos, turn_sin = turn_tables
    blocks = signal.reshape(signal.shape[0], outer, inner)
    first_re = jnp.einsum("kn,cnm->ckm", cos_out, blocks, precision=HIGHEST_MODE)
    first_im = -jnp.einsum("kn,cnm->ckm", sin_out, blocks, precision=HIGHEST_MODE)
    turned_re = first_re * turn_cos + first_im * turn_sin
    turned_im = first_im * turn_cos - first_re * turn_sin
    real_part = jnp.einsum("ckm,mj->ckj", turned_re, cos_in, precision=HIGHEST_MODE) + jnp.einsum(
        "ckm,mj->ckj", turned_im, sin_in, precision=HIGHEST_MODE
    )
    imag_part = jnp.einsum("ckm,mj->ckj", turned_im, cos_in, precision=HIGHEST_MODE) - jnp.einsum(
        "ckm,mj->ckj", turned_re, sin_in, precision=HIGHEST_MODE
    )
    return (real_part, imag_part)


def long_convolution(mixed, filters, gains):
    channels, length = mixed.shape
    inner, outer = split_factor(length)
    total = 2 * length
    outer_tables = tables(outer)
    inner_tables = tables(inner)
    turn_tables = twiddle(outer, inner, total)
    signal = mixed.astype(jnp.float32)
    padding = jnp.zeros((channels, length), jnp.float32)
    sig_re, sig_im = spectrum(
        jnp.concatenate([signal, padding], 1), inner, outer, outer_tables, inner_tables, turn_tables
    )
    fil_re, fil_im = spectrum(
        jnp.concatenate([filters, padding], 1),
        inner,
        outer,
        outer_tables,
        inner_tables,
        turn_tables,
    )
    prod_re = sig_re * fil_re - sig_im * fil_im
    prod_im = sig_re * fil_im + sig_im * fil_re
    cos_in, sin_in = inner_tables
    back_re = jnp.einsum("ckj,jm->ckm", prod_re, cos_in, precision=HIGHEST_MODE) - jnp.einsum(
        "ckj,jm->ckm", prod_im, sin_in, precision=HIGHEST_MODE
    )
    back_im = jnp.einsum("ckj,jm->ckm", prod_re, sin_in, precision=HIGHEST_MODE) + jnp.einsum(
        "ckj,jm->ckm", prod_im, cos_in, precision=HIGHEST_MODE
    )
    turn_cos, turn_sin = turn_tables
    rot_re = back_re * turn_cos - back_im * turn_sin
    rot_im = back_re * turn_sin + back_im * turn_cos
    cos_out, sin_out = outer_tables
    half = outer // 2
    result = jnp.einsum("nk,ckm->cnm", cos_out[:half], rot_re, precision=HIGHEST_MODE) - jnp.einsum(
        "nk,ckm->cnm", sin_out[:half], rot_im, precision=HIGHEST_MODE
    )
    return result.reshape(channels, length) / total + gains[:, None] * signal


def shifted_filter(current, tail, taps):
    span = taps.shape[0]
    rows = current.shape[0]
    joined = jnp.concatenate([tail, current], 0).astype(jnp.float32)
    total = taps[0] * joined[span - 1 :]
    for offset in range(1, span):
        total = total + taps[offset] * joined[span - 1 - offset : span - 1 - offset + rows]
    return total


def body(queries, keys, values, short_taps, long_filter, skip_gain, out_weight):
    rows, width = queries.shape
    span = short_taps.shape[1]
    edge = rows - (span - 1)
    tails = shifted(jnp.stack([queries[edge:], keys[edge:], values[edge:]]), "seq", 1)
    short_q = shifted_filter(queries, tails[0], short_taps[0]).astype(jnp.bfloat16)
    mixed = (
        shifted_filter(keys, tails[1], short_taps[1])
        * shifted_filter(values, tails[2], short_taps[2])
    ).astype(jnp.bfloat16)
    groups = lax.axis_size("seq")
    per_group = width // groups
    mixed_t = mixed.T.reshape(groups, per_group, rows)
    split_mixed = lax.all_to_all(mixed_t, "seq", split_axis=0, concat_axis=0, tiled=True)
    signal = split_mixed.transpose(1, 0, 2).reshape(per_group, groups * rows)
    convolved = long_convolution(signal, long_filter, skip_gain).astype(jnp.bfloat16)
    outgoing = convolved.reshape(per_group, groups, rows).transpose(1, 0, 2)
    returned = lax.all_to_all(outgoing, "seq", split_axis=0, concat_axis=0, tiled=True)
    long_out = returned.reshape(width, rows).T
    gated = (short_q.astype(jnp.float32) * long_out.astype(jnp.float32)).astype(jnp.bfloat16)
    pieces = lax.all_gather(gated, "chan", axis=0, tiled=False)
    weight = out_weight.reshape(pieces.shape[0], width, out_weight.shape[1])
    result = jnp.einsum("gtc,gcj->tj", pieces, weight, preferred_element_type=jnp.float32)
    return result.astype(jnp.bfloat16)


def solution(mesh):
    in_specs = (
        P("seq", "chan"),
        P("seq", "chan"),
        P("seq", "chan"),
        P(None, None, "chan"),
        P(("chan", "seq"), None),
        P(("chan", "seq")),
        P(None, "chan"),
    )
    out_specs = P("seq", "chan")
    return jax.shard_map(body, mesh=mesh, in_specs=in_specs, out_specs=out_specs, check_vma=False)
```

```python
import math

import jax
import jax.numpy as jnp
from jax import lax
from jax.sharding import PartitionSpec as P

HIGHEST_MODE = lax.Precision.HIGHEST


def shifted(block, axis, distance):
    devices = range(lax.axis_size(axis))
    route = [(i - distance, i) for i in devices if i - distance in devices]
    return lax.ppermute(block, axis, route)


def tables(count):
    index = jnp.arange(count, dtype=jnp.int32)
    phase = (index[:, None] * index[None, :] % count).astype(jnp.float32) * (2.0 * math.pi / count)
    return (jnp.cos(phase), jnp.sin(phase))


def twiddle(outer, inner, total):
    first = jnp.arange(outer, dtype=jnp.int32)
    second = jnp.arange(inner, dtype=jnp.int32)
    phase = (first[:, None] * second[None, :] % total).astype(jnp.float32) * (2.0 * math.pi / total)
    return (jnp.cos(phase), jnp.sin(phase))


def split_factor(length):
    total = 2 * length
    best = 1
    candidate = 1
    while candidate * candidate <= total:
        if length % candidate == 0:
            best = candidate
        candidate += 1
    return (best, total // best)


def spectrum(signal, inner, outer, outer_tables, inner_tables, turn_tables):
    cos_out, sin_out = outer_tables
    cos_in, sin_in = inner_tables
    turn_cos, turn_sin = turn_tables
    blocks = signal.reshape(signal.shape[0], outer, inner)
    first_re = jnp.einsum("kn,cnm->ckm", cos_out, blocks, precision=HIGHEST_MODE)
    first_im = -jnp.einsum("kn,cnm->ckm", sin_out, blocks, precision=HIGHEST_MODE)
    turned_re = first_re * turn_cos + first_im * turn_sin
    turned_im = first_im * turn_cos - first_re * turn_sin
    real_part = jnp.einsum("ckm,mj->ckj", turned_re, cos_in, precision=HIGHEST_MODE) + jnp.einsum(
        "ckm,mj->ckj", turned_im, sin_in, precision=HIGHEST_MODE
    )
    imag_part = jnp.einsum("ckm,mj->ckj", turned_im, cos_in, precision=HIGHEST_MODE) - jnp.einsum(
        "ckm,mj->ckj", turned_re, sin_in, precision=HIGHEST_MODE
    )
    return (real_part, imag_part)


def long_convolution(mixed, filters, gains):
    channels, length = mixed.shape
    inner, outer = split_factor(length)
    total = 2 * length
    outer_tables = tables(outer)
    inner_tables = tables(inner)
    turn_tables = twiddle(outer, inner, total)
    signal = mixed.astype(jnp.float32)
    padding = jnp.zeros((channels, length), jnp.float32)
    sig_re, sig_im = spectrum(
        jnp.concatenate([signal, padding], 1), inner, outer, outer_tables, inner_tables, turn_tables
    )
    fil_re, fil_im = spectrum(
        jnp.concatenate([filters, padding], 1),
        inner,
        outer,
        outer_tables,
        inner_tables,
        turn_tables,
    )
    prod_re = sig_re * fil_re - sig_im * fil_im
    prod_im = sig_re * fil_im + sig_im * fil_re
    cos_in, sin_in = inner_tables
    back_re = jnp.einsum("ckj,jm->ckm", prod_re, cos_in, precision=HIGHEST_MODE) - jnp.einsum(
        "ckj,jm->ckm", prod_im, sin_in, precision=HIGHEST_MODE
    )
    back_im = jnp.einsum("ckj,jm->ckm", prod_re, sin_in, precision=HIGHEST_MODE) + jnp.einsum(
        "ckj,jm->ckm", prod_im, cos_in, precision=HIGHEST_MODE
    )
    turn_cos, turn_sin = turn_tables
    rot_re = back_re * turn_cos - back_im * turn_sin
    rot_im = back_re * turn_sin + back_im * turn_cos
    cos_out, sin_out = outer_tables
    half = outer // 2
    result = jnp.einsum("nk,ckm->cnm", cos_out[:half], rot_re, precision=HIGHEST_MODE) - jnp.einsum(
        "nk,ckm->cnm", sin_out[:half], rot_im, precision=HIGHEST_MODE
    )
    return result.reshape(channels, length) / total + gains[:, None] * signal


def shifted_filter(current, tail, taps):
    span = taps.shape[0]
    rows = current.shape[0]
    joined = jnp.concatenate([tail, current], 0).astype(jnp.float32)
    total = taps[0] * joined[span - 1 :]
    for offset in range(1, span):
        total = total + taps[offset] * joined[span - 1 - offset : span - 1 - offset + rows]
    return total


def chan_route(size, step):
    pairs = size // 2
    return [(x * 2 + h, ((x + step) % pairs) * 2 + h) for x in range(pairs) for h in range(2)]


def gather_chan(block):
    size = lax.axis_size("chan")
    pairs = size // 2
    me = lax.axis_index("chan")
    mine_x = me // 2
    mine_h = me % 2
    partner = lax.ppermute(block, "chan", [(i, i ^ 1) for i in range(size)])
    held = jnp.stack([block, partner])
    slots = [held]
    places = [mine_x]
    right = held
    left = held
    for step in range(1, pairs // 2 + 1):
        right = lax.ppermute(right, "chan", chan_route(size, 1))
        slots.append(right)
        places.append((mine_x - step) % pairs)
        if step < pairs - step:
            left = lax.ppermute(left, "chan", chan_route(size, -1))
            slots.append(left)
            places.append((mine_x + step) % pairs)
    place = jnp.stack(places)
    order = jnp.stack([place * 2 + mine_h, place * 2 + (1 - mine_h)], axis=1)
    return jnp.stack(slots), order


def body(queries, keys, values, short_taps, long_filter, skip_gain, out_weight):
    rows, width = queries.shape
    span = short_taps.shape[1]
    edge = rows - (span - 1)
    tails = shifted(jnp.stack([queries[edge:], keys[edge:], values[edge:]]), "seq", 1)
    short_q = shifted_filter(queries, tails[0], short_taps[0]).astype(jnp.bfloat16)
    mixed = (
        shifted_filter(keys, tails[1], short_taps[1])
        * shifted_filter(values, tails[2], short_taps[2])
    ).astype(jnp.bfloat16)
    groups = lax.axis_size("seq")
    per_group = width // groups
    mixed_t = mixed.T.reshape(groups, per_group, rows)
    split_mixed = lax.all_to_all(mixed_t, "seq", split_axis=0, concat_axis=0, tiled=True)
    signal = split_mixed.transpose(1, 0, 2).reshape(per_group, groups * rows)
    convolved = long_convolution(signal, long_filter, skip_gain).astype(jnp.bfloat16)
    outgoing = convolved.reshape(per_group, groups, rows).transpose(1, 0, 2)
    returned = lax.all_to_all(outgoing, "seq", split_axis=0, concat_axis=0, tiled=True)
    long_out = returned.reshape(width, rows).T
    gated = (short_q.astype(jnp.float32) * long_out.astype(jnp.float32)).astype(jnp.bfloat16)
    pieces, order = gather_chan(gated)
    weight = out_weight.reshape(-1, width, out_weight.shape[1])[order]
    result = jnp.einsum("pqtc,pqcj->tj", pieces, weight, preferred_element_type=jnp.float32)
    return result.astype(jnp.bfloat16)


def solution(mesh):
    in_specs = (
        P("seq", "chan"),
        P("seq", "chan"),
        P("seq", "chan"),
        P(None, None, "chan"),
        P(("chan", "seq"), None),
        P(("chan", "seq")),
        P(None, "chan"),
    )
    out_specs = P("seq", "chan")
    return jax.shard_map(body, mesh=mesh, in_specs=in_specs, out_specs=out_specs, check_vma=False)
```

```python
import math

import jax
import jax.numpy as jnp
from jax import lax
from jax.sharding import PartitionSpec as P

HIGHEST_MODE = lax.Precision.HIGHEST


def shifted(block, axis, distance):
    devices = range(lax.axis_size(axis))
    route = [(i - distance, i) for i in devices if i - distance in devices]
    return lax.ppermute(block, axis, route)


def tables(count):
    index = jnp.arange(count, dtype=jnp.int32)
    phase = (index[:, None] * index[None, :] % count).astype(jnp.float32) * (2.0 * math.pi / count)
    return (jnp.cos(phase), jnp.sin(phase))


def twiddle(outer, inner, total):
    first = jnp.arange(outer, dtype=jnp.int32)
    second = jnp.arange(inner, dtype=jnp.int32)
    phase = (first[:, None] * second[None, :] % total).astype(jnp.float32) * (2.0 * math.pi / total)
    return (jnp.cos(phase), jnp.sin(phase))


def split_factor(length):
    total = 2 * length
    best = 1
    candidate = 1
    while candidate * candidate <= total:
        if length % candidate == 0:
            best = candidate
        candidate += 1
    return (best, total // best)


def spectrum(signal, inner, outer, outer_tables, inner_tables, turn_tables):
    cos_out, sin_out = outer_tables
    cos_in, sin_in = inner_tables
    turn_cos, turn_sin = turn_tables
    blocks = signal.reshape(signal.shape[0], outer, inner)
    first_re = jnp.einsum("kn,cnm->ckm", cos_out, blocks, precision=HIGHEST_MODE)
    first_im = -jnp.einsum("kn,cnm->ckm", sin_out, blocks, precision=HIGHEST_MODE)
    turned_re = first_re * turn_cos + first_im * turn_sin
    turned_im = first_im * turn_cos - first_re * turn_sin
    real_part = jnp.einsum("ckm,mj->ckj", turned_re, cos_in, precision=HIGHEST_MODE) + jnp.einsum(
        "ckm,mj->ckj", turned_im, sin_in, precision=HIGHEST_MODE
    )
    imag_part = jnp.einsum("ckm,mj->ckj", turned_im, cos_in, precision=HIGHEST_MODE) - jnp.einsum(
        "ckm,mj->ckj", turned_re, sin_in, precision=HIGHEST_MODE
    )
    return (real_part, imag_part)


def long_convolution(mixed, filters, gains):
    channels, length = mixed.shape
    inner, outer = split_factor(length)
    total = 2 * length
    outer_tables = tables(outer)
    inner_tables = tables(inner)
    turn_tables = twiddle(outer, inner, total)
    signal = mixed.astype(jnp.float32)
    padding = jnp.zeros((channels, length), jnp.float32)
    sig_re, sig_im = spectrum(
        jnp.concatenate([signal, padding], 1), inner, outer, outer_tables, inner_tables, turn_tables
    )
    fil_re, fil_im = spectrum(
        jnp.concatenate([filters, padding], 1),
        inner,
        outer,
        outer_tables,
        inner_tables,
        turn_tables,
    )
    prod_re = sig_re * fil_re - sig_im * fil_im
    prod_im = sig_re * fil_im + sig_im * fil_re
    cos_in, sin_in = inner_tables
    back_re = jnp.einsum("ckj,jm->ckm", prod_re, cos_in, precision=HIGHEST_MODE) - jnp.einsum(
        "ckj,jm->ckm", prod_im, sin_in, precision=HIGHEST_MODE
    )
    back_im = jnp.einsum("ckj,jm->ckm", prod_re, sin_in, precision=HIGHEST_MODE) + jnp.einsum(
        "ckj,jm->ckm", prod_im, cos_in, precision=HIGHEST_MODE
    )
    turn_cos, turn_sin = turn_tables
    rot_re = back_re * turn_cos - back_im * turn_sin
    rot_im = back_re * turn_sin + back_im * turn_cos
    cos_out, sin_out = outer_tables
    half = outer // 2
    result = jnp.einsum("nk,ckm->cnm", cos_out[:half], rot_re, precision=HIGHEST_MODE) - jnp.einsum(
        "nk,ckm->cnm", sin_out[:half], rot_im, precision=HIGHEST_MODE
    )
    return result.reshape(channels, length) / total + gains[:, None] * signal


def shifted_filter(current, tail, taps):
    span = taps.shape[0]
    rows = current.shape[0]
    joined = jnp.concatenate([tail, current], 0).astype(jnp.float32)
    total = taps[0] * joined[span - 1 :]
    for offset in range(1, span):
        total = total + taps[offset] * joined[span - 1 - offset : span - 1 - offset + rows]
    return total


def chan_route(size, step):
    pairs = size // 2
    return [(x * 2 + h, ((x + step) % pairs) * 2 + h) for x in range(pairs) for h in range(2)]


def gather_chan(block):
    size = lax.axis_size("chan")
    pairs = size // 2
    me = lax.axis_index("chan")
    mine_x = me // 2
    mine_h = me % 2
    partner = lax.ppermute(block, "chan", [(i, i ^ 1) for i in range(size)])
    held = jnp.stack([block, partner])
    slots = [held]
    places = [mine_x]
    right = held
    left = held
    for step in range(1, pairs // 2 + 1):
        right = lax.ppermute(right, "chan", chan_route(size, 1))
        slots.append(right)
        places.append((mine_x - step) % pairs)
        if step < pairs - step:
            left = lax.ppermute(left, "chan", chan_route(size, -1))
            slots.append(left)
            places.append((mine_x + step) % pairs)
    place = jnp.stack(places)
    order = jnp.stack([place * 2 + mine_h, place * 2 + (1 - mine_h)], axis=1)
    return jnp.stack(slots), order


def body(queries, keys, values, short_taps, long_filter, skip_gain, out_weight):
    rows, width = queries.shape
    span = short_taps.shape[1]
    edge = rows - (span - 1)
    tails = shifted(jnp.stack([queries[edge:], keys[edge:], values[edge:]]), "seq", 1)
    short_q = shifted_filter(queries, tails[0], short_taps[0]).astype(jnp.bfloat16)
    mixed = (
        shifted_filter(keys, tails[1], short_taps[1])
        * shifted_filter(values, tails[2], short_taps[2])
    ).astype(jnp.bfloat16)
    groups = lax.axis_size("seq")
    per_group = width // groups
    mixed_t = mixed.T.reshape(groups, per_group, rows)
    split_mixed = lax.all_to_all(mixed_t, "seq", split_axis=0, concat_axis=0, tiled=True)
    signal = split_mixed.transpose(1, 0, 2).reshape(per_group, groups * rows)
    convolved = long_convolution(signal, long_filter, skip_gain).astype(jnp.bfloat16)
    outgoing = convolved.reshape(per_group, groups, rows).transpose(1, 0, 2)
    returned = lax.all_to_all(outgoing, "seq", split_axis=0, concat_axis=0, tiled=True)
    long_out = returned.reshape(width, rows).T
    gated = (short_q.astype(jnp.float32) * long_out.astype(jnp.float32)).astype(jnp.bfloat16)
    size = lax.axis_size("chan")
    pieces = lax.all_to_all(
        jnp.broadcast_to(gated[None], (size,) + gated.shape), "chan", split_axis=0, concat_axis=0, tiled=True
    )
    weight = out_weight.reshape(size, width, out_weight.shape[1])
    result = jnp.einsum("gtc,gcj->tj", pieces, weight, preferred_element_type=jnp.float32)
    return result.astype(jnp.bfloat16)


def solution(mesh):
    in_specs = (
        P("seq", "chan"),
        P("seq", "chan"),
        P("seq", "chan"),
        P(None, None, "chan"),
        P(("chan", "seq"), None),
        P(("chan", "seq")),
        P(None, "chan"),
    )
    out_specs = P("seq", "chan")
    return jax.shard_map(body, mesh=mesh, in_specs=in_specs, out_specs=out_specs, check_vma=False)
```

```python
import math

import jax
import jax.numpy as jnp
from jax import lax
from jax.sharding import Mesh, PartitionSpec as P

HIGHEST_MODE = lax.Precision.HIGHEST


def shifted(block, axis, distance):
    devices = range(lax.axis_size(axis))
    route = [(i - distance, i) for i in devices if i - distance in devices]
    return lax.ppermute(block, axis, route)


def tables(count):
    index = jnp.arange(count, dtype=jnp.int32)
    phase = (index[:, None] * index[None, :] % count).astype(jnp.float32) * (2.0 * math.pi / count)
    return (jnp.cos(phase), jnp.sin(phase))


def twiddle(outer, inner, total):
    first = jnp.arange(outer, dtype=jnp.int32)
    second = jnp.arange(inner, dtype=jnp.int32)
    phase = (first[:, None] * second[None, :] % total).astype(jnp.float32) * (2.0 * math.pi / total)
    return (jnp.cos(phase), jnp.sin(phase))


def split_factor(length):
    total = 2 * length
    best = 1
    candidate = 1
    while candidate * candidate <= total:
        if length % candidate == 0:
            best = candidate
        candidate += 1
    return (best, total // best)


def spectrum(signal, inner, outer, outer_tables, inner_tables, turn_tables):
    cos_out, sin_out = outer_tables
    cos_in, sin_in = inner_tables
    turn_cos, turn_sin = turn_tables
    blocks = signal.reshape(signal.shape[0], outer, inner)
    first_re = jnp.einsum("kn,cnm->ckm", cos_out, blocks, precision=HIGHEST_MODE)
    first_im = -jnp.einsum("kn,cnm->ckm", sin_out, blocks, precision=HIGHEST_MODE)
    turned_re = first_re * turn_cos + first_im * turn_sin
    turned_im = first_im * turn_cos - first_re * turn_sin
    real_part = jnp.einsum("ckm,mj->ckj", turned_re, cos_in, precision=HIGHEST_MODE) + jnp.einsum(
        "ckm,mj->ckj", turned_im, sin_in, precision=HIGHEST_MODE
    )
    imag_part = jnp.einsum("ckm,mj->ckj", turned_im, cos_in, precision=HIGHEST_MODE) - jnp.einsum(
        "ckm,mj->ckj", turned_re, sin_in, precision=HIGHEST_MODE
    )
    return (real_part, imag_part)


def long_convolution(mixed, filters, gains):
    channels, length = mixed.shape
    inner, outer = split_factor(length)
    total = 2 * length
    outer_tables = tables(outer)
    inner_tables = tables(inner)
    turn_tables = twiddle(outer, inner, total)
    signal = mixed.astype(jnp.float32)
    padding = jnp.zeros((channels, length), jnp.float32)
    sig_re, sig_im = spectrum(
        jnp.concatenate([signal, padding], 1), inner, outer, outer_tables, inner_tables, turn_tables
    )
    fil_re, fil_im = spectrum(
        jnp.concatenate([filters, padding], 1),
        inner,
        outer,
        outer_tables,
        inner_tables,
        turn_tables,
    )
    prod_re = sig_re * fil_re - sig_im * fil_im
    prod_im = sig_re * fil_im + sig_im * fil_re
    cos_in, sin_in = inner_tables
    back_re = jnp.einsum("ckj,jm->ckm", prod_re, cos_in, precision=HIGHEST_MODE) - jnp.einsum(
        "ckj,jm->ckm", prod_im, sin_in, precision=HIGHEST_MODE
    )
    back_im = jnp.einsum("ckj,jm->ckm", prod_re, sin_in, precision=HIGHEST_MODE) + jnp.einsum(
        "ckj,jm->ckm", prod_im, cos_in, precision=HIGHEST_MODE
    )
    turn_cos, turn_sin = turn_tables
    rot_re = back_re * turn_cos - back_im * turn_sin
    rot_im = back_re * turn_sin + back_im * turn_cos
    cos_out, sin_out = outer_tables
    half = outer // 2
    result = jnp.einsum("nk,ckm->cnm", cos_out[:half], rot_re, precision=HIGHEST_MODE) - jnp.einsum(
        "nk,ckm->cnm", sin_out[:half], rot_im, precision=HIGHEST_MODE
    )
    return result.reshape(channels, length) / total + gains[:, None] * signal


def shifted_filter(current, tail, taps):
    span = taps.shape[0]
    rows = current.shape[0]
    joined = jnp.concatenate([tail, current], 0).astype(jnp.float32)
    total = taps[0] * joined[span - 1 :]
    for offset in range(1, span):
        total = total + taps[offset] * joined[span - 1 - offset : span - 1 - offset + rows]
    return total


SEQ = ("z", "ylo", "core")
CHAN = ("x", "yh")


def swap_half(block):
    return lax.ppermute(block, "yh", [(0, 1), (1, 0)])


def body(queries, keys, values, short_taps, long_filter, skip_gain, out_weight):
    rows, width = queries.shape
    span = short_taps.shape[1]
    edge = rows - (span - 1)
    planes = lax.axis_size("x")
    half = lax.axis_index("yh")
    groups = lax.axis_size(SEQ)
    seq_index = lax.axis_index(SEQ)
    columns = out_weight.shape[1]
    by_group = out_weight.reshape(planes, 2, width, columns)
    other_rows = lax.dynamic_index_in_dim(by_group, 1 - half, axis=1, keepdims=False)
    piece_rows = other_rows.reshape(planes * width, columns)
    chunk = piece_rows.shape[0] // groups
    sent_piece = lax.dynamic_slice_in_dim(piece_rows, seq_index * chunk, chunk, axis=0)
    partner_piece = swap_half(sent_piece)
    partner_weight = lax.all_gather(partner_piece, SEQ, axis=0, tiled=True)
    tails = shifted(jnp.stack([queries[edge:], keys[edge:], values[edge:]]), SEQ, 1)
    short_q = shifted_filter(queries, tails[0], short_taps[0]).astype(jnp.bfloat16)
    mixed = (
        shifted_filter(keys, tails[1], short_taps[1])
        * shifted_filter(values, tails[2], short_taps[2])
    ).astype(jnp.bfloat16)
    per_group = width // groups
    mixed_t = mixed.T.reshape(groups, per_group, rows)
    split_mixed = lax.all_to_all(mixed_t, SEQ, split_axis=0, concat_axis=0, tiled=True)
    signal = split_mixed.transpose(1, 0, 2).reshape(per_group, groups * rows)
    convolved = long_convolution(signal, long_filter, skip_gain).astype(jnp.bfloat16)
    outgoing = convolved.reshape(per_group, groups, rows).transpose(1, 0, 2)
    returned = lax.all_to_all(outgoing, SEQ, split_axis=0, concat_axis=0, tiled=True)
    long_out = returned.reshape(width, rows).T
    gated = (short_q.astype(jnp.float32) * long_out.astype(jnp.float32)).astype(jnp.bfloat16)
    pieces = lax.all_to_all(
        jnp.broadcast_to(gated[None], (planes,) + gated.shape), "x", split_axis=0, concat_axis=0, tiled=True
    )
    own_rows = lax.dynamic_index_in_dim(by_group, half, axis=1, keepdims=False)
    own_part = jnp.einsum("gtc,gcj->tj", pieces, own_rows, preferred_element_type=jnp.float32)
    other_part = jnp.einsum(
        "gtc,gcj->tj", pieces, partner_weight.reshape(planes, width, columns), preferred_element_type=jnp.float32
    )
    result = own_part + swap_half(other_part)
    return result.astype(jnp.bfloat16)


def solution(mesh):
    shape = mesh.devices.shape
    fine = Mesh(mesh.devices.reshape(shape[0] // 8, 4, 2, shape[1] // 2, 2), SEQ + CHAN)
    in_specs = (
        P(SEQ, CHAN),
        P(SEQ, CHAN),
        P(SEQ, CHAN),
        P(None, None, CHAN),
        P(CHAN + SEQ, None),
        P(CHAN + SEQ),
        P(None, CHAN),
    )
    out_specs = P(SEQ, CHAN)
    return jax.shard_map(body, mesh=fine, in_specs=in_specs, out_specs=out_specs, check_vma=False)
```

```python
import math

import jax
import jax.numpy as jnp
from jax import lax
from jax.sharding import PartitionSpec as P

HIGHEST_MODE = lax.Precision.HIGHEST


def shifted(block, axis, distance):
    devices = range(lax.axis_size(axis))
    route = [(i - distance, i) for i in devices if i - distance in devices]
    return lax.ppermute(block, axis, route)


def tables(count):
    index = jnp.arange(count, dtype=jnp.int32)
    phase = (index[:, None] * index[None, :] % count).astype(jnp.float32) * (2.0 * math.pi / count)
    return (jnp.cos(phase), jnp.sin(phase))


def twiddle(outer, inner, total):
    first = jnp.arange(outer, dtype=jnp.int32)
    second = jnp.arange(inner, dtype=jnp.int32)
    phase = (first[:, None] * second[None, :] % total).astype(jnp.float32) * (2.0 * math.pi / total)
    return (jnp.cos(phase), jnp.sin(phase))


def split_factor(length):
    total = 2 * length
    best = 1
    candidate = 1
    while candidate * candidate <= total:
        if length % candidate == 0:
            best = candidate
        candidate += 1
    return (best, total // best)


def spectrum(signal, inner, outer, outer_tables, inner_tables, turn_tables):
    cos_out, sin_out = outer_tables
    cos_in, sin_in = inner_tables
    turn_cos, turn_sin = turn_tables
    blocks = signal.reshape(signal.shape[0], outer, inner)
    first_re = jnp.einsum("kn,cnm->ckm", cos_out, blocks, precision=HIGHEST_MODE)
    first_im = -jnp.einsum("kn,cnm->ckm", sin_out, blocks, precision=HIGHEST_MODE)
    turned_re = first_re * turn_cos + first_im * turn_sin
    turned_im = first_im * turn_cos - first_re * turn_sin
    real_part = jnp.einsum("ckm,mj->ckj", turned_re, cos_in, precision=HIGHEST_MODE) + jnp.einsum(
        "ckm,mj->ckj", turned_im, sin_in, precision=HIGHEST_MODE
    )
    imag_part = jnp.einsum("ckm,mj->ckj", turned_im, cos_in, precision=HIGHEST_MODE) - jnp.einsum(
        "ckm,mj->ckj", turned_re, sin_in, precision=HIGHEST_MODE
    )
    return (real_part, imag_part)


def long_convolution(mixed, filters, gains):
    channels, length = mixed.shape
    inner, outer = split_factor(length)
    total = 2 * length
    outer_tables = tables(outer)
    inner_tables = tables(inner)
    turn_tables = twiddle(outer, inner, total)
    signal = mixed.astype(jnp.float32)
    padding = jnp.zeros((channels, length), jnp.float32)
    sig_re, sig_im = spectrum(
        jnp.concatenate([signal, padding], 1), inner, outer, outer_tables, inner_tables, turn_tables
    )
    fil_re, fil_im = spectrum(
        jnp.concatenate([filters, padding], 1),
        inner,
        outer,
        outer_tables,
        inner_tables,
        turn_tables,
    )
    prod_re = sig_re * fil_re - sig_im * fil_im
    prod_im = sig_re * fil_im + sig_im * fil_re
    cos_in, sin_in = inner_tables
    back_re = jnp.einsum("ckj,jm->ckm", prod_re, cos_in, precision=HIGHEST_MODE) - jnp.einsum(
        "ckj,jm->ckm", prod_im, sin_in, precision=HIGHEST_MODE
    )
    back_im = jnp.einsum("ckj,jm->ckm", prod_re, sin_in, precision=HIGHEST_MODE) + jnp.einsum(
        "ckj,jm->ckm", prod_im, cos_in, precision=HIGHEST_MODE
    )
    turn_cos, turn_sin = turn_tables
    rot_re = back_re * turn_cos - back_im * turn_sin
    rot_im = back_re * turn_sin + back_im * turn_cos
    cos_out, sin_out = outer_tables
    half = outer // 2
    result = jnp.einsum("nk,ckm->cnm", cos_out[:half], rot_re, precision=HIGHEST_MODE) - jnp.einsum(
        "nk,ckm->cnm", sin_out[:half], rot_im, precision=HIGHEST_MODE
    )
    return result.reshape(channels, length) / total + gains[:, None] * signal


def shifted_filter(current, tail, taps):
    span = taps.shape[0]
    rows = current.shape[0]
    joined = jnp.concatenate([tail, current], 0).astype(jnp.float32)
    total = taps[0] * joined[span - 1 :]
    for offset in range(1, span):
        total = total + taps[offset] * joined[span - 1 - offset : span - 1 - offset + rows]
    return total


def chan_route(size, step):
    pairs = size // 2
    return [(x * 2 + h, ((x + step) % pairs) * 2 + h) for x in range(pairs) for h in range(2)]


def gather_chan(block):
    size = lax.axis_size("chan")
    pairs = size // 2
    me = lax.axis_index("chan")
    mine_x = me // 2
    mine_h = me % 2
    partner = lax.ppermute(block, "chan", [(i, i ^ 1) for i in range(size)])
    moving = jnp.stack([block, partner])
    slots = [moving]
    places = [mine_x]
    for step in range(1, pairs):
        moving = lax.ppermute(moving, "chan", chan_route(size, 1))
        slots.append(moving)
        places.append((mine_x - step) % pairs)
    place = jnp.stack(places)
    order = jnp.stack([place * 2 + mine_h, place * 2 + (1 - mine_h)], axis=1)
    return jnp.stack(slots), order


def causal_filter(signal, taps):
    length = signal.shape[-1]
    total = taps[0][:, None] * signal
    for offset in range(1, taps.shape[0]):
        moved = jnp.concatenate(
            [jnp.zeros(signal.shape[:-1] + (offset,), signal.dtype), signal[..., : length - offset]], -1
        )
        total = total + taps[offset][:, None] * moved
    return total


def body(queries, keys, values, short_taps, long_filter, skip_gain, out_weight):
    rows, width = queries.shape
    span = short_taps.shape[1]
    edge = rows - (span - 1)
    groups = lax.axis_size("seq")
    per_group = width // groups
    seq_index = lax.axis_index("seq")
    raw = jnp.stack([keys.T, values.T]).reshape(2, groups, per_group, rows).transpose(1, 0, 2, 3)
    split_raw = lax.all_to_all(raw, "seq", split_axis=0, concat_axis=0, tiled=True)
    whole = split_raw.transpose(1, 2, 0, 3).reshape(2, per_group, groups * rows).astype(jnp.float32)
    own_taps = lax.dynamic_slice_in_dim(short_taps, seq_index * per_group, per_group, axis=2)
    signal = (causal_filter(whole[0], own_taps[1]) * causal_filter(whole[1], own_taps[2])).astype(jnp.bfloat16)
    tail = shifted(queries[edge:], "seq", 1)
    short_q = shifted_filter(queries, tail, short_taps[0]).astype(jnp.bfloat16)
    convolved = long_convolution(signal, long_filter, skip_gain).astype(jnp.bfloat16)
    outgoing = convolved.reshape(per_group, groups, rows).transpose(1, 0, 2)
    returned = lax.all_to_all(outgoing, "seq", split_axis=0, concat_axis=0, tiled=True)
    long_out = returned.reshape(width, rows).T
    gated = (short_q.astype(jnp.float32) * long_out.astype(jnp.float32)).astype(jnp.bfloat16)
    pieces, order = gather_chan(gated)
    weight = out_weight.reshape(-1, width, out_weight.shape[1])[order]
    result = jnp.einsum("pqtc,pqcj->tj", pieces, weight, preferred_element_type=jnp.float32)
    return result.astype(jnp.bfloat16)


def solution(mesh):
    in_specs = (
        P("seq", "chan"),
        P("seq", "chan"),
        P("seq", "chan"),
        P(None, None, "chan"),
        P(("chan", "seq"), None),
        P(("chan", "seq")),
        P(None, "chan"),
    )
    out_specs = P("seq", "chan")
    return jax.shard_map(body, mesh=mesh, in_specs=in_specs, out_specs=out_specs, check_vma=False)
```

```python
import math

import jax
import jax.numpy as jnp
from jax import lax
from jax.sharding import PartitionSpec as P

HIGHEST_MODE = lax.Precision.HIGHEST


def shifted(block, axis, distance):
    devices = range(lax.axis_size(axis))
    route = [(i - distance, i) for i in devices if i - distance in devices]
    return lax.ppermute(block, axis, route)


def tables(count):
    index = jnp.arange(count, dtype=jnp.int32)
    phase = (index[:, None] * index[None, :] % count).astype(jnp.float32) * (2.0 * math.pi / count)
    return (jnp.cos(phase), jnp.sin(phase))


def twiddle(outer, inner, total):
    first = jnp.arange(outer, dtype=jnp.int32)
    second = jnp.arange(inner, dtype=jnp.int32)
    phase = (first[:, None] * second[None, :] % total).astype(jnp.float32) * (2.0 * math.pi / total)
    return (jnp.cos(phase), jnp.sin(phase))


def split_factor(length):
    total = 2 * length
    best = 1
    candidate = 1
    while candidate * candidate <= total:
        if length % candidate == 0:
            best = candidate
        candidate += 1
    return (best, total // best)


def spectrum(signal, inner, outer, outer_tables, inner_tables, turn_tables):
    cos_out, sin_out = outer_tables
    cos_in, sin_in = inner_tables
    turn_cos, turn_sin = turn_tables
    blocks = signal.reshape(signal.shape[0], outer, inner)
    first_re = jnp.einsum("kn,cnm->ckm", cos_out, blocks, precision=HIGHEST_MODE)
    first_im = -jnp.einsum("kn,cnm->ckm", sin_out, blocks, precision=HIGHEST_MODE)
    turned_re = first_re * turn_cos + first_im * turn_sin
    turned_im = first_im * turn_cos - first_re * turn_sin
    real_part = jnp.einsum("ckm,mj->ckj", turned_re, cos_in, precision=HIGHEST_MODE) + jnp.einsum(
        "ckm,mj->ckj", turned_im, sin_in, precision=HIGHEST_MODE
    )
    imag_part = jnp.einsum("ckm,mj->ckj", turned_im, cos_in, precision=HIGHEST_MODE) - jnp.einsum(
        "ckm,mj->ckj", turned_re, sin_in, precision=HIGHEST_MODE
    )
    return (real_part, imag_part)


def long_convolution(mixed, filters, gains):
    channels, length = mixed.shape
    inner, outer = split_factor(length)
    total = 2 * length
    outer_tables = tables(outer)
    inner_tables = tables(inner)
    turn_tables = twiddle(outer, inner, total)
    signal = mixed.astype(jnp.float32)
    padding = jnp.zeros((channels, length), jnp.float32)
    sig_re, sig_im = spectrum(
        jnp.concatenate([signal, padding], 1), inner, outer, outer_tables, inner_tables, turn_tables
    )
    fil_re, fil_im = spectrum(
        jnp.concatenate([filters, padding], 1),
        inner,
        outer,
        outer_tables,
        inner_tables,
        turn_tables,
    )
    prod_re = sig_re * fil_re - sig_im * fil_im
    prod_im = sig_re * fil_im + sig_im * fil_re
    cos_in, sin_in = inner_tables
    back_re = jnp.einsum("ckj,jm->ckm", prod_re, cos_in, precision=HIGHEST_MODE) - jnp.einsum(
        "ckj,jm->ckm", prod_im, sin_in, precision=HIGHEST_MODE
    )
    back_im = jnp.einsum("ckj,jm->ckm", prod_re, sin_in, precision=HIGHEST_MODE) + jnp.einsum(
        "ckj,jm->ckm", prod_im, cos_in, precision=HIGHEST_MODE
    )
    turn_cos, turn_sin = turn_tables
    rot_re = back_re * turn_cos - back_im * turn_sin
    rot_im = back_re * turn_sin + back_im * turn_cos
    cos_out, sin_out = outer_tables
    half = outer // 2
    result = jnp.einsum("nk,ckm->cnm", cos_out[:half], rot_re, precision=HIGHEST_MODE) - jnp.einsum(
        "nk,ckm->cnm", sin_out[:half], rot_im, precision=HIGHEST_MODE
    )
    return result.reshape(channels, length) / total + gains[:, None] * signal


def shifted_filter(current, tail, taps):
    span = taps.shape[0]
    rows = current.shape[0]
    joined = jnp.concatenate([tail, current], 0).astype(jnp.float32)
    total = taps[0] * joined[span - 1 :]
    for offset in range(1, span):
        total = total + taps[offset] * joined[span - 1 - offset : span - 1 - offset + rows]
    return total


def chan_route(size, step):
    pairs = size // 2
    return [(x * 2 + h, ((x + step) % pairs) * 2 + h) for x in range(pairs) for h in range(2)]


def gather_chan(block):
    size = lax.axis_size("chan")
    pairs = size // 2
    me = lax.axis_index("chan")
    mine_x = me // 2
    mine_h = me % 2
    partner = lax.ppermute(block, "chan", [(i, i ^ 1) for i in range(size)])
    shifts = [d for d in range(1 - pairs // 2, pairs // 2 + 1) if d != 0]
    own = [block] + [lax.ppermute(block, "chan", chan_route(size, d)) for d in shifts]
    other = [partner] + [lax.ppermute(partner, "chan", chan_route(size, d)) for d in shifts]
    place = jnp.stack([mine_x] + [(mine_x - d) % pairs for d in shifts])
    order = jnp.concatenate([place * 2 + mine_h, place * 2 + (1 - mine_h)])
    return jnp.stack(own + other), order


def body(queries, keys, values, short_taps, long_filter, skip_gain, out_weight):
    rows, width = queries.shape
    span = short_taps.shape[1]
    edge = rows - (span - 1)
    tails = shifted(jnp.stack([queries[edge:], keys[edge:], values[edge:]]), "seq", 1)
    short_q = shifted_filter(queries, tails[0], short_taps[0]).astype(jnp.bfloat16)
    mixed = (
        shifted_filter(keys, tails[1], short_taps[1])
        * shifted_filter(values, tails[2], short_taps[2])
    ).astype(jnp.bfloat16)
    groups = lax.axis_size("seq")
    per_group = width // groups
    mixed_t = mixed.T.reshape(groups, per_group, rows)
    split_mixed = lax.all_to_all(mixed_t, "seq", split_axis=0, concat_axis=0, tiled=True)
    signal = split_mixed.transpose(1, 0, 2).reshape(per_group, groups * rows)
    convolved = long_convolution(signal, long_filter, skip_gain).astype(jnp.bfloat16)
    outgoing = convolved.reshape(per_group, groups, rows).transpose(1, 0, 2)
    returned = lax.all_to_all(outgoing, "seq", split_axis=0, concat_axis=0, tiled=True)
    long_out = returned.reshape(width, rows).T
    gated = (short_q.astype(jnp.float32) * long_out.astype(jnp.float32)).astype(jnp.bfloat16)
    pieces, order = gather_chan(gated)
    weight = out_weight.reshape(-1, width, out_weight.shape[1])[order]
    result = jnp.einsum("gtc,gcj->tj", pieces, weight, preferred_element_type=jnp.float32)
    return result.astype(jnp.bfloat16)


def solution(mesh):
    in_specs = (
        P("seq", "chan"),
        P("seq", "chan"),
        P("seq", "chan"),
        P(None, None, "chan"),
        P(("chan", "seq"), None),
        P(("chan", "seq")),
        P(None, "chan"),
    )
    out_specs = P("seq", "chan")
    return jax.shard_map(body, mesh=mesh, in_specs=in_specs, out_specs=out_specs, check_vma=False)
```

```python
import math

import jax
import jax.numpy as jnp
from jax import lax
from jax.sharding import PartitionSpec as P

HIGHEST_MODE = lax.Precision.HIGHEST


def tables(count):
    index = jnp.arange(count, dtype=jnp.int32)
    phase = (index[:, None] * index[None, :] % count).astype(jnp.float32) * (2.0 * math.pi / count)
    return (jnp.cos(phase), jnp.sin(phase))


def twiddle(outer, inner, total):
    first = jnp.arange(outer, dtype=jnp.int32)
    second = jnp.arange(inner, dtype=jnp.int32)
    phase = (first[:, None] * second[None, :] % total).astype(jnp.float32) * (2.0 * math.pi / total)
    return (jnp.cos(phase), jnp.sin(phase))


def split_factor(length):
    total = 2 * length
    best = 1
    candidate = 1
    while candidate * candidate <= total:
        if length % candidate == 0:
            best = candidate
        candidate += 1
    return (best, total // best)


def spectrum(signal, inner, outer, outer_tables, inner_tables, turn_tables):
    cos_out, sin_out = outer_tables
    cos_in, sin_in = inner_tables
    turn_cos, turn_sin = turn_tables
    blocks = signal.reshape(signal.shape[0], outer, inner)
    first_re = jnp.einsum("kn,cnm->ckm", cos_out, blocks, precision=HIGHEST_MODE)
    first_im = -jnp.einsum("kn,cnm->ckm", sin_out, blocks, precision=HIGHEST_MODE)
    turned_re = first_re * turn_cos + first_im * turn_sin
    turned_im = first_im * turn_cos - first_re * turn_sin
    real_part = jnp.einsum("ckm,mj->ckj", turned_re, cos_in, precision=HIGHEST_MODE) + jnp.einsum(
        "ckm,mj->ckj", turned_im, sin_in, precision=HIGHEST_MODE
    )
    imag_part = jnp.einsum("ckm,mj->ckj", turned_im, cos_in, precision=HIGHEST_MODE) - jnp.einsum(
        "ckm,mj->ckj", turned_re, sin_in, precision=HIGHEST_MODE
    )
    return (real_part, imag_part)


def long_convolution(mixed, filters, gains):
    channels, length = mixed.shape
    inner, outer = split_factor(length)
    total = 2 * length
    outer_tables = tables(outer)
    inner_tables = tables(inner)
    turn_tables = twiddle(outer, inner, total)
    signal = mixed.astype(jnp.float32)
    padding = jnp.zeros((channels, length), jnp.float32)
    sig_re, sig_im = spectrum(
        jnp.concatenate([signal, padding], 1), inner, outer, outer_tables, inner_tables, turn_tables
    )
    fil_re, fil_im = spectrum(
        jnp.concatenate([filters, padding], 1),
        inner,
        outer,
        outer_tables,
        inner_tables,
        turn_tables,
    )
    prod_re = sig_re * fil_re - sig_im * fil_im
    prod_im = sig_re * fil_im + sig_im * fil_re
    cos_in, sin_in = inner_tables
    back_re = jnp.einsum("ckj,jm->ckm", prod_re, cos_in, precision=HIGHEST_MODE) - jnp.einsum(
        "ckj,jm->ckm", prod_im, sin_in, precision=HIGHEST_MODE
    )
    back_im = jnp.einsum("ckj,jm->ckm", prod_re, sin_in, precision=HIGHEST_MODE) + jnp.einsum(
        "ckj,jm->ckm", prod_im, cos_in, precision=HIGHEST_MODE
    )
    turn_cos, turn_sin = turn_tables
    rot_re = back_re * turn_cos - back_im * turn_sin
    rot_im = back_re * turn_sin + back_im * turn_cos
    cos_out, sin_out = outer_tables
    half = outer // 2
    result = jnp.einsum("nk,ckm->cnm", cos_out[:half], rot_re, precision=HIGHEST_MODE) - jnp.einsum(
        "nk,ckm->cnm", sin_out[:half], rot_im, precision=HIGHEST_MODE
    )
    return result.reshape(channels, length) / total + gains[:, None] * signal


def chan_route(size, step):
    pairs = size // 2
    return [(x * 2 + h, ((x + step) % pairs) * 2 + h) for x in range(pairs) for h in range(2)]


def gather_chan(block):
    size = lax.axis_size("chan")
    pairs = size // 2
    me = lax.axis_index("chan")
    mine_x = me // 2
    mine_h = me % 2
    partner = lax.ppermute(block, "chan", [(i, i ^ 1) for i in range(size)])
    held = jnp.stack([block, partner])
    slots = [held]
    places = [mine_x]
    right = held
    left = held
    for step in range(1, pairs // 2 + 1):
        right = lax.ppermute(right, "chan", chan_route(size, 1))
        slots.append(right)
        places.append((mine_x - step) % pairs)
        if step < pairs - step:
            left = lax.ppermute(left, "chan", chan_route(size, -1))
            slots.append(left)
            places.append((mine_x + step) % pairs)
    place = jnp.stack(places)
    order = jnp.stack([place * 2 + mine_h, place * 2 + (1 - mine_h)], axis=1)
    return jnp.stack(slots), order


def causal_filter(signal, taps):
    length = signal.shape[-1]
    total = taps[0][:, None] * signal
    for offset in range(1, taps.shape[0]):
        moved = jnp.concatenate(
            [jnp.zeros(signal.shape[:-1] + (offset,), signal.dtype), signal[..., : length - offset]], -1
        )
        total = total + taps[offset][:, None] * moved
    return total


def body(queries, keys, values, short_taps, long_filter, skip_gain, out_weight):
    rows, width = queries.shape
    groups = lax.axis_size("seq")
    per_group = width // groups
    seq_index = lax.axis_index("seq")
    raw = jnp.stack([queries.T, keys.T, values.T]).reshape(3, groups, per_group, rows).transpose(1, 0, 2, 3)
    split_raw = lax.all_to_all(raw, "seq", split_axis=0, concat_axis=0, tiled=True)
    whole = split_raw.transpose(1, 2, 0, 3).reshape(3, per_group, groups * rows).astype(jnp.float32)
    own_taps = lax.dynamic_slice_in_dim(short_taps, seq_index * per_group, per_group, axis=2)
    short_q = causal_filter(whole[0], own_taps[0]).astype(jnp.bfloat16)
    signal = (causal_filter(whole[1], own_taps[1]) * causal_filter(whole[2], own_taps[2])).astype(jnp.bfloat16)
    convolved = long_convolution(signal, long_filter, skip_gain).astype(jnp.bfloat16)
    gated_t = (short_q.astype(jnp.float32) * convolved.astype(jnp.float32)).astype(jnp.bfloat16)
    outgoing = gated_t.reshape(per_group, groups, rows).transpose(1, 0, 2)
    returned = lax.all_to_all(outgoing, "seq", split_axis=0, concat_axis=0, tiled=True)
    gated = returned.reshape(width, rows).T
    pieces, order = gather_chan(gated)
    weight = out_weight.reshape(-1, width, out_weight.shape[1])[order]
    result = jnp.einsum("pqtc,pqcj->tj", pieces, weight, preferred_element_type=jnp.float32)
    return result.astype(jnp.bfloat16)


def solution(mesh):
    in_specs = (
        P("seq", "chan"),
        P("seq", "chan"),
        P("seq", "chan"),
        P(None, None, "chan"),
        P(("chan", "seq"), None),
        P(("chan", "seq")),
        P(None, "chan"),
    )
    out_specs = P("seq", "chan")
    return jax.shard_map(body, mesh=mesh, in_specs=in_specs, out_specs=out_specs, check_vma=False)
```

```python
import math

import jax
import jax.numpy as jnp
from jax import lax
from jax.sharding import Mesh, PartitionSpec as P

HIGHEST_MODE = lax.Precision.HIGHEST


def tables(count):
    index = jnp.arange(count, dtype=jnp.int32)
    phase = (index[:, None] * index[None, :] % count).astype(jnp.float32) * (2.0 * math.pi / count)
    return (jnp.cos(phase), jnp.sin(phase))


def twiddle(outer, inner, total):
    first = jnp.arange(outer, dtype=jnp.int32)
    second = jnp.arange(inner, dtype=jnp.int32)
    phase = (first[:, None] * second[None, :] % total).astype(jnp.float32) * (2.0 * math.pi / total)
    return (jnp.cos(phase), jnp.sin(phase))


def split_factor(length):
    total = 2 * length
    best = 1
    candidate = 1
    while candidate * candidate <= total:
        if length % candidate == 0:
            best = candidate
        candidate += 1
    return (best, total // best)


def spectrum(signal, inner, outer, outer_tables, inner_tables, turn_tables):
    cos_out, sin_out = outer_tables
    cos_in, sin_in = inner_tables
    turn_cos, turn_sin = turn_tables
    blocks = signal.reshape(signal.shape[0], outer, inner)
    first_re = jnp.einsum("kn,cnm->ckm", cos_out, blocks, precision=HIGHEST_MODE)
    first_im = -jnp.einsum("kn,cnm->ckm", sin_out, blocks, precision=HIGHEST_MODE)
    turned_re = first_re * turn_cos + first_im * turn_sin
    turned_im = first_im * turn_cos - first_re * turn_sin
    real_part = jnp.einsum("ckm,mj->ckj", turned_re, cos_in, precision=HIGHEST_MODE) + jnp.einsum(
        "ckm,mj->ckj", turned_im, sin_in, precision=HIGHEST_MODE
    )
    imag_part = jnp.einsum("ckm,mj->ckj", turned_im, cos_in, precision=HIGHEST_MODE) - jnp.einsum(
        "ckm,mj->ckj", turned_re, sin_in, precision=HIGHEST_MODE
    )
    return (real_part, imag_part)


def long_convolution(mixed, filters, gains):
    channels, length = mixed.shape
    inner, outer = split_factor(length)
    total = 2 * length
    outer_tables = tables(outer)
    inner_tables = tables(inner)
    turn_tables = twiddle(outer, inner, total)
    signal = mixed.astype(jnp.float32)
    padding = jnp.zeros((channels, length), jnp.float32)
    sig_re, sig_im = spectrum(
        jnp.concatenate([signal, padding], 1), inner, outer, outer_tables, inner_tables, turn_tables
    )
    fil_re, fil_im = spectrum(
        jnp.concatenate([filters, padding], 1),
        inner,
        outer,
        outer_tables,
        inner_tables,
        turn_tables,
    )
    prod_re = sig_re * fil_re - sig_im * fil_im
    prod_im = sig_re * fil_im + sig_im * fil_re
    cos_in, sin_in = inner_tables
    back_re = jnp.einsum("ckj,jm->ckm", prod_re, cos_in, precision=HIGHEST_MODE) - jnp.einsum(
        "ckj,jm->ckm", prod_im, sin_in, precision=HIGHEST_MODE
    )
    back_im = jnp.einsum("ckj,jm->ckm", prod_re, sin_in, precision=HIGHEST_MODE) + jnp.einsum(
        "ckj,jm->ckm", prod_im, cos_in, precision=HIGHEST_MODE
    )
    turn_cos, turn_sin = turn_tables
    rot_re = back_re * turn_cos - back_im * turn_sin
    rot_im = back_re * turn_sin + back_im * turn_cos
    cos_out, sin_out = outer_tables
    half = outer // 2
    result = jnp.einsum("nk,ckm->cnm", cos_out[:half], rot_re, precision=HIGHEST_MODE) - jnp.einsum(
        "nk,ckm->cnm", sin_out[:half], rot_im, precision=HIGHEST_MODE
    )
    return result.reshape(channels, length) / total + gains[:, None] * signal


def gather_pairs(held):
    size = lax.axis_size("x")
    mine = lax.axis_index("x")
    slots = [held]
    places = [mine]
    right = held
    left = held
    for step in range(1, size // 2 + 1):
        right = lax.ppermute(right, "x", [(i, (i + 1) % size) for i in range(size)])
        slots.append(right)
        places.append((mine - step) % size)
        if step < size - step:
            left = lax.ppermute(left, "x", [(i, (i - 1) % size) for i in range(size)])
            slots.append(left)
            places.append((mine + step) % size)
    place = jnp.stack(places)
    order = jnp.stack([place * 2, place * 2 + 1], axis=1)
    return jnp.stack(slots), order


def causal_filter(signal, taps):
    length = signal.shape[-1]
    total = taps[0][:, None] * signal
    for offset in range(1, taps.shape[0]):
        moved = jnp.concatenate(
            [jnp.zeros(signal.shape[:-1] + (offset,), signal.dtype), signal[..., : length - offset]], -1
        )
        total = total + taps[offset][:, None] * moved
    return total


def body(queries, keys, values, short_taps, long_filter, skip_gain, out_weight):
    rows, width = queries.shape
    groups = lax.axis_size(SEQ)
    per_group = width // groups
    seq_index = lax.axis_index(SEQ)
    raw = jnp.stack([queries.T, keys.T, values.T]).reshape(3, groups, per_group, rows).transpose(1, 0, 2, 3)
    split_raw = lax.all_to_all(raw, SEQ, split_axis=0, concat_axis=0, tiled=True)
    whole = split_raw.transpose(1, 2, 0, 3).reshape(3, per_group, groups * rows).astype(jnp.float32)
    own_taps = lax.dynamic_slice_in_dim(short_taps, seq_index * per_group, per_group, axis=2)
    short_q = causal_filter(whole[0], own_taps[0]).astype(jnp.bfloat16)
    signal = (causal_filter(whole[1], own_taps[1]) * causal_filter(whole[2], own_taps[2])).astype(jnp.bfloat16)
    convolved = long_convolution(signal, long_filter, skip_gain).astype(jnp.bfloat16)
    gated_t = (short_q.astype(jnp.float32) * convolved.astype(jnp.float32)).astype(jnp.bfloat16)
    outgoing = gated_t.reshape(per_group, groups, rows).transpose(1, 0, 2)
    both = jnp.broadcast_to(outgoing[None], (2,) + outgoing.shape).reshape((2 * groups,) + outgoing.shape[1:])
    returned = lax.all_to_all(both, ("yh",) + SEQ, split_axis=0, concat_axis=0, tiled=True)
    held = returned.reshape(2, width, rows).transpose(0, 2, 1)
    pieces, order = gather_pairs(held)
    weight = out_weight.reshape(-1, width, out_weight.shape[1])[order]
    result = jnp.einsum("pqtc,pqcj->tj", pieces, weight, preferred_element_type=jnp.float32)
    return result.astype(jnp.bfloat16)


SEQ = ("z", "ylo", "core")
CHAN = ("x", "yh")


def solution(mesh):
    shape = mesh.devices.shape
    fine = Mesh(mesh.devices.reshape(shape[0] // 8, 4, 2, shape[1] // 2, 2), SEQ + CHAN)
    in_specs = (
        P(SEQ, CHAN),
        P(SEQ, CHAN),
        P(SEQ, CHAN),
        P(None, None, CHAN),
        P(CHAN + SEQ, None),
        P(CHAN + SEQ),
        P(None, CHAN),
    )
    out_specs = P(SEQ, CHAN)
    return jax.shard_map(body, mesh=fine, in_specs=in_specs, out_specs=out_specs, check_vma=False)
```

```python
import math

import jax
import jax.numpy as jnp
from jax import lax
from jax.sharding import Mesh, PartitionSpec as P

HIGHEST_MODE = lax.Precision.HIGHEST


def tables(count):
    index = jnp.arange(count, dtype=jnp.int32)
    phase = (index[:, None] * index[None, :] % count).astype(jnp.float32) * (2.0 * math.pi / count)
    return (jnp.cos(phase), jnp.sin(phase))


def twiddle(outer, inner, total):
    first = jnp.arange(outer, dtype=jnp.int32)
    second = jnp.arange(inner, dtype=jnp.int32)
    phase = (first[:, None] * second[None, :] % total).astype(jnp.float32) * (2.0 * math.pi / total)
    return (jnp.cos(phase), jnp.sin(phase))


def split_factor(length):
    total = 2 * length
    best = 1
    candidate = 1
    while candidate * candidate <= total:
        if length % candidate == 0:
            best = candidate
        candidate += 1
    return (best, total // best)


def rotation(cos_t, sin_t, sign):
    return jnp.concatenate(
        [jnp.concatenate([cos_t, sign * sin_t], 1), jnp.concatenate([-sign * sin_t, cos_t], 1)], 0
    )


def spectrum(signal, inner, outer, outer_tables, inner_tables, turn_tables):
    cos_out, sin_out = outer_tables
    cos_in, sin_in = inner_tables
    turn_cos, turn_sin = turn_tables
    used = signal.shape[1] // inner
    blocks = signal.reshape(signal.shape[0], used, inner)
    stacked = jnp.concatenate([cos_out[:, :used], -sin_out[:, :used]], 0)
    first = jnp.einsum("kn,cnm->ckm", stacked, blocks, precision=HIGHEST_MODE)
    first_re, first_im = first[:, :outer], first[:, outer:]
    turned_re = first_re * turn_cos + first_im * turn_sin
    turned_im = first_im * turn_cos - first_re * turn_sin
    turned = jnp.concatenate([turned_re, turned_im], 2)
    second = jnp.einsum("ckm,mj->ckj", turned, rotation(cos_in, sin_in, -1.0), precision=HIGHEST_MODE)
    return (second[..., :inner], second[..., inner:])


def long_convolution(mixed, filters, gains):
    channels, length = mixed.shape
    inner, outer = split_factor(length)
    total = 2 * length
    outer_tables = tables(outer)
    inner_tables = tables(inner)
    turn_tables = twiddle(outer, inner, total)
    signal = mixed.astype(jnp.float32)
    sig_re, sig_im = spectrum(signal, inner, outer, outer_tables, inner_tables, turn_tables)
    fil_re, fil_im = spectrum(filters, inner, outer, outer_tables, inner_tables, turn_tables)
    prod_re = sig_re * fil_re - sig_im * fil_im
    prod_im = sig_re * fil_im + sig_im * fil_re
    cos_in, sin_in = inner_tables
    product = jnp.concatenate([prod_re, prod_im], 2)
    back = jnp.einsum("ckj,jm->ckm", product, rotation(cos_in, sin_in, 1.0), precision=HIGHEST_MODE)
    back_re, back_im = back[..., :inner], back[..., inner:]
    turn_cos, turn_sin = turn_tables
    rot_re = back_re * turn_cos - back_im * turn_sin
    rot_im = back_re * turn_sin + back_im * turn_cos
    cos_out, sin_out = outer_tables
    half = outer // 2
    stacked = jnp.concatenate([cos_out[:half], -sin_out[:half]], 1)
    result = jnp.einsum("nk,ckm->cnm", stacked, jnp.concatenate([rot_re, rot_im], 1), precision=HIGHEST_MODE)
    return result.reshape(channels, length) / total + gains[:, None] * signal


def gather_pairs(held):
    size = lax.axis_size("x")
    mine = lax.axis_index("x")
    slots = [held]
    places = [mine]
    right = held
    left = held
    for step in range(1, size // 2 + 1):
        right = lax.ppermute(right, "x", [(i, (i + 1) % size) for i in range(size)])
        slots.append(right)
        places.append((mine - step) % size)
        if step < size - step:
            left = lax.ppermute(left, "x", [(i, (i - 1) % size) for i in range(size)])
            slots.append(left)
            places.append((mine + step) % size)
    place = jnp.stack(places)
    order = jnp.stack([place * 2, place * 2 + 1], axis=1)
    return jnp.stack(slots), order


def causal_filter(signal, taps):
    length = signal.shape[-1]
    total = taps[0][:, None] * signal
    for offset in range(1, taps.shape[0]):
        moved = jnp.concatenate(
            [jnp.zeros(signal.shape[:-1] + (offset,), signal.dtype), signal[..., : length - offset]], -1
        )
        total = total + taps[offset][:, None] * moved
    return total


def body(queries, keys, values, short_taps, long_filter, skip_gain, out_weight):
    rows, width = queries.shape
    groups = lax.axis_size(SEQ)
    per_group = width // groups
    seq_index = lax.axis_index(SEQ)
    raw = jnp.stack([queries.T, keys.T, values.T]).reshape(3, groups, per_group, rows).transpose(1, 0, 2, 3)
    split_raw = lax.all_to_all(raw, SEQ, split_axis=0, concat_axis=0, tiled=True)
    whole = split_raw.transpose(1, 2, 0, 3).reshape(3, per_group, groups * rows).astype(jnp.float32)
    own_taps = lax.dynamic_slice_in_dim(short_taps, seq_index * per_group, per_group, axis=2)
    short_q = causal_filter(whole[0], own_taps[0]).astype(jnp.bfloat16)
    signal = (causal_filter(whole[1], own_taps[1]) * causal_filter(whole[2], own_taps[2])).astype(jnp.bfloat16)
    convolved = long_convolution(signal, long_filter, skip_gain).astype(jnp.bfloat16)
    gated_t = (short_q.astype(jnp.float32) * convolved.astype(jnp.float32)).astype(jnp.bfloat16)
    outgoing = gated_t.reshape(per_group, groups, rows).transpose(1, 0, 2)
    both = jnp.broadcast_to(outgoing[None], (2,) + outgoing.shape).reshape((2 * groups,) + outgoing.shape[1:])
    returned = lax.all_to_all(both, ("yh",) + SEQ, split_axis=0, concat_axis=0, tiled=True)
    held = returned.reshape(2, width, rows).transpose(0, 2, 1)
    pieces, order = gather_pairs(held)
    weight = out_weight.reshape(-1, width, out_weight.shape[1])[order]
    result = jnp.einsum("pqtc,pqcj->tj", pieces, weight, preferred_element_type=jnp.float32)
    return result.astype(jnp.bfloat16)


SEQ = ("z", "ylo", "core")
CHAN = ("x", "yh")


def solution(mesh):
    shape = mesh.devices.shape
    fine = Mesh(mesh.devices.reshape(shape[0] // 8, 4, 2, shape[1] // 2, 2), SEQ + CHAN)
    in_specs = (
        P(SEQ, CHAN),
        P(SEQ, CHAN),
        P(SEQ, CHAN),
        P(None, None, CHAN),
        P(CHAN + SEQ, None),
        P(CHAN + SEQ),
        P(None, CHAN),
    )
    out_specs = P(SEQ, CHAN)
    return jax.shard_map(body, mesh=fine, in_specs=in_specs, out_specs=out_specs, check_vma=False)
```

```python
import math

import jax
import jax.numpy as jnp
from jax import lax
from jax.sharding import Mesh, PartitionSpec as P

HIGHEST_MODE = lax.Precision.HIGHEST


def tables(count):
    index = jnp.arange(count, dtype=jnp.int32)
    phase = (index[:, None] * index[None, :] % count).astype(jnp.float32) * (2.0 * math.pi / count)
    return (jnp.cos(phase), jnp.sin(phase))


def twiddle(outer, inner, total):
    first = jnp.arange(outer, dtype=jnp.int32)
    second = jnp.arange(inner, dtype=jnp.int32)
    phase = (first[:, None] * second[None, :] % total).astype(jnp.float32) * (2.0 * math.pi / total)
    return (jnp.cos(phase), jnp.sin(phase))


def split_factor(length):
    total = 2 * length
    best = 1
    candidate = 1
    while candidate * candidate <= total:
        if length % candidate == 0:
            best = candidate
        candidate += 1
    return (best, total // best)


def rotation(cos_t, sin_t, sign):
    return jnp.concatenate(
        [jnp.concatenate([cos_t, sign * sin_t], 1), jnp.concatenate([-sign * sin_t, cos_t], 1)], 0
    )


def spectrum(signal, inner, outer, outer_tables, inner_tables, turn_tables):
    cos_out, sin_out = outer_tables
    cos_in, sin_in = inner_tables
    turn_cos, turn_sin = turn_tables
    used = signal.shape[1] // inner
    blocks = signal.reshape(signal.shape[0], used, inner)
    stacked = jnp.concatenate([cos_out[:, :used], -sin_out[:, :used]], 0)
    first = jnp.einsum("kn,cnm->ckm", stacked, blocks, precision=HIGHEST_MODE)
    first_re, first_im = first[:, :outer], first[:, outer:]
    turned_re = first_re * turn_cos + first_im * turn_sin
    turned_im = first_im * turn_cos - first_re * turn_sin
    turned = jnp.concatenate([turned_re, turned_im], 2)
    second = jnp.einsum("ckm,mj->ckj", turned, rotation(cos_in, sin_in, -1.0), precision=HIGHEST_MODE)
    return (second[..., :inner], second[..., inner:])


def long_convolution(mixed, filters, gains):
    channels, length = mixed.shape
    inner, outer = split_factor(length)
    total = 2 * length
    outer_tables = tables(outer)
    inner_tables = tables(inner)
    turn_tables = twiddle(outer, inner, total)
    signal = mixed.astype(jnp.float32)
    sig_re, sig_im = spectrum(signal, inner, outer, outer_tables, inner_tables, turn_tables)
    fil_re, fil_im = spectrum(filters, inner, outer, outer_tables, inner_tables, turn_tables)
    prod_re = sig_re * fil_re - sig_im * fil_im
    prod_im = sig_re * fil_im + sig_im * fil_re
    cos_in, sin_in = inner_tables
    product = jnp.concatenate([prod_re, prod_im], 2)
    back = jnp.einsum("ckj,jm->ckm", product, rotation(cos_in, sin_in, 1.0), precision=HIGHEST_MODE)
    back_re, back_im = back[..., :inner], back[..., inner:]
    turn_cos, turn_sin = turn_tables
    rot_re = back_re * turn_cos - back_im * turn_sin
    rot_im = back_re * turn_sin + back_im * turn_cos
    cos_out, sin_out = outer_tables
    half = outer // 2
    stacked = jnp.concatenate([cos_out[:half], -sin_out[:half]], 1)
    result = jnp.einsum("nk,ckm->cnm", stacked, jnp.concatenate([rot_re, rot_im], 1), precision=HIGHEST_MODE)
    return result.reshape(channels, length) / total + gains[:, None] * signal


def gather_quads(held):
    size = lax.axis_size(X)
    half = size // 2
    mine = lax.axis_index(X)
    right = lax.ppermute(held, X, [(i, (i + 1) % size) for i in range(size)])
    left = lax.ppermute(held, X, [(i, (i - 1) % size) for i in range(size)])
    farther = lax.ppermute(right, X, [(i, (i + 1) % size) for i in range(size)])
    origins = jnp.stack([mine, (mine - 1) % size, (mine + 1) % size, (mine - 2) % size])
    places = (origins % half)[:, None] + half * jnp.arange(2)[None, :]
    order = places[:, :, None] * 2 + jnp.arange(2)[None, None, :]
    return jnp.stack([held, right, left, farther]), order


def causal_filter(signal, taps):
    length = signal.shape[-1]
    total = taps[0][:, None] * signal
    for offset in range(1, taps.shape[0]):
        moved = jnp.concatenate(
            [jnp.zeros(signal.shape[:-1] + (offset,), signal.dtype), signal[..., : length - offset]], -1
        )
        total = total + taps[offset][:, None] * moved
    return total


def body(queries, keys, values, short_taps, long_filter, skip_gain, out_weight):
    rows, width = queries.shape
    groups = lax.axis_size(SEQ)
    per_group = width // groups
    seq_index = lax.axis_index(SEQ)
    raw = jnp.stack([queries.T, keys.T, values.T]).reshape(3, groups, per_group, rows).transpose(1, 0, 2, 3)
    split_raw = lax.all_to_all(raw, SEQ, split_axis=0, concat_axis=0, tiled=True)
    whole = split_raw.transpose(1, 2, 0, 3).reshape(3, per_group, groups * rows).astype(jnp.float32)
    own_taps = lax.dynamic_slice_in_dim(short_taps, seq_index * per_group, per_group, axis=2)
    short_q = causal_filter(whole[0], own_taps[0]).astype(jnp.bfloat16)
    signal = (causal_filter(whole[1], own_taps[1]) * causal_filter(whole[2], own_taps[2])).astype(jnp.bfloat16)
    convolved = long_convolution(signal, long_filter, skip_gain).astype(jnp.bfloat16)
    gated_t = (short_q.astype(jnp.float32) * convolved.astype(jnp.float32)).astype(jnp.bfloat16)
    outgoing = gated_t.reshape(per_group, groups, rows).transpose(1, 0, 2)
    copies = jnp.broadcast_to(outgoing[None], (4,) + outgoing.shape).reshape((4 * groups,) + outgoing.shape[1:])
    returned = lax.all_to_all(copies, ("xhi", "yh") + SEQ, split_axis=0, concat_axis=0, tiled=True)
    held = returned.reshape(2, 2, width, rows).transpose(0, 1, 3, 2)
    pieces, order = gather_quads(held)
    weight = out_weight.reshape(-1, width, out_weight.shape[1])[order]
    result = jnp.einsum("sahtc,sahcj->tj", pieces, weight, preferred_element_type=jnp.float32)
    return result.astype(jnp.bfloat16)


SEQ = ("z", "ylo", "core")
X = ("xhi", "xlo")
CHAN = X + ("yh",)


def solution(mesh):
    shape = mesh.devices.shape
    fine = Mesh(mesh.devices.reshape(shape[0] // 8, 4, 2, 2, shape[1] // 4, 2), SEQ + CHAN)
    in_specs = (
        P(SEQ, CHAN),
        P(SEQ, CHAN),
        P(SEQ, CHAN),
        P(None, None, CHAN),
        P(CHAN + SEQ, None),
        P(CHAN + SEQ),
        P(None, CHAN),
    )
    out_specs = P(SEQ, CHAN)
    return jax.shard_map(body, mesh=fine, in_specs=in_specs, out_specs=out_specs, check_vma=False)
```

```python
import math

import jax
import jax.numpy as jnp
from jax import lax
from jax.sharding import Mesh, PartitionSpec as P

HIGHEST_MODE = lax.Precision.HIGHEST


def tables(count):
    index = jnp.arange(count, dtype=jnp.int32)
    phase = (index[:, None] * index[None, :] % count).astype(jnp.float32) * (2.0 * math.pi / count)
    return (jnp.cos(phase), jnp.sin(phase))


def twiddle(outer, inner, total):
    first = jnp.arange(outer, dtype=jnp.int32)
    second = jnp.arange(inner, dtype=jnp.int32)
    phase = (first[:, None] * second[None, :] % total).astype(jnp.float32) * (2.0 * math.pi / total)
    return (jnp.cos(phase), jnp.sin(phase))


def split_factor(length):
    total = 2 * length
    best = 1
    candidate = 1
    while candidate * candidate <= total:
        if length % candidate == 0:
            best = candidate
        candidate += 1
    return (best, total // best)


def rotation(cos_t, sin_t, sign):
    return jnp.concatenate(
        [jnp.concatenate([cos_t, sign * sin_t], 1), jnp.concatenate([-sign * sin_t, cos_t], 1)], 0
    )


def spectrum(signal, inner, outer, outer_tables, inner_tables, turn_tables):
    cos_out, sin_out = outer_tables
    cos_in, sin_in = inner_tables
    turn_cos, turn_sin = turn_tables
    used = signal.shape[1] // inner
    blocks = signal.reshape(signal.shape[0], used, inner)
    stacked = jnp.concatenate([cos_out[:, :used], -sin_out[:, :used]], 0)
    first = jnp.einsum("kn,cnm->ckm", stacked, blocks, precision=HIGHEST_MODE)
    first_re, first_im = first[:, :outer], first[:, outer:]
    turned_re = first_re * turn_cos + first_im * turn_sin
    turned_im = first_im * turn_cos - first_re * turn_sin
    turned = jnp.concatenate([turned_re, turned_im], 2)
    second = jnp.einsum("ckm,mj->ckj", turned, rotation(cos_in, sin_in, -1.0), precision=HIGHEST_MODE)
    return (second[..., :inner], second[..., inner:])


def long_convolution(mixed, filters, gains):
    channels, length = mixed.shape
    inner, outer = split_factor(length)
    total = 2 * length
    outer_tables = tables(outer)
    inner_tables = tables(inner)
    turn_tables = twiddle(outer, inner, total)
    signal = mixed.astype(jnp.float32)
    sig_re, sig_im = spectrum(signal, inner, outer, outer_tables, inner_tables, turn_tables)
    fil_re, fil_im = spectrum(filters, inner, outer, outer_tables, inner_tables, turn_tables)
    prod_re = sig_re * fil_re - sig_im * fil_im
    prod_im = sig_re * fil_im + sig_im * fil_re
    cos_in, sin_in = inner_tables
    product = jnp.concatenate([prod_re, prod_im], 2)
    back = jnp.einsum("ckj,jm->ckm", product, rotation(cos_in, sin_in, 1.0), precision=HIGHEST_MODE)
    back_re, back_im = back[..., :inner], back[..., inner:]
    turn_cos, turn_sin = turn_tables
    rot_re = back_re * turn_cos - back_im * turn_sin
    rot_im = back_re * turn_sin + back_im * turn_cos
    cos_out, sin_out = outer_tables
    half = outer // 2
    stacked = jnp.concatenate([cos_out[:half], -sin_out[:half]], 1)
    result = jnp.einsum("nk,ckm->cnm", stacked, jnp.concatenate([rot_re, rot_im], 1), precision=HIGHEST_MODE)
    return result.reshape(channels, length) / total + gains[:, None] * signal


def gather_pairs(held):
    size = lax.axis_size("x")
    mine = lax.axis_index("x")

    def moved(block, step):
        return lax.ppermute(block, "x", [(i, (i + step) % size) for i in range(size)])

    right = moved(held, 1)
    left = moved(held, -1)
    across = moved(held, size // 2)
    right_two = moved(jnp.stack([right, held]), 2)
    left_two = moved(jnp.stack([left, held]), -2)
    pieces = jnp.concatenate([jnp.stack([held, right, left, across]), right_two, left_two])
    offsets = jnp.array([0, -1, 1, -(size // 2), -3, -2, 3, 2], jnp.int32)
    place = (mine + offsets) % size
    order = jnp.stack([place * 2, place * 2 + 1], axis=1)
    return pieces, order


def causal_filter(signal, taps):
    length = signal.shape[-1]
    total = taps[0][:, None] * signal
    for offset in range(1, taps.shape[0]):
        moved = jnp.concatenate(
            [jnp.zeros(signal.shape[:-1] + (offset,), signal.dtype), signal[..., : length - offset]], -1
        )
        total = total + taps[offset][:, None] * moved
    return total


def body(queries, keys, values, short_taps, long_filter, skip_gain, out_weight):
    rows, width = queries.shape
    groups = lax.axis_size(SEQ)
    per_group = width // groups
    seq_index = lax.axis_index(SEQ)
    raw = jnp.stack([queries.T, keys.T, values.T]).reshape(3, groups, per_group, rows).transpose(1, 0, 2, 3)
    split_raw = lax.all_to_all(raw, SEQ, split_axis=0, concat_axis=0, tiled=True)
    whole = split_raw.transpose(1, 2, 0, 3).reshape(3, per_group, groups * rows).astype(jnp.float32)
    own_taps = lax.dynamic_slice_in_dim(short_taps, seq_index * per_group, per_group, axis=2)
    short_q = causal_filter(whole[0], own_taps[0]).astype(jnp.bfloat16)
    signal = (causal_filter(whole[1], own_taps[1]) * causal_filter(whole[2], own_taps[2])).astype(jnp.bfloat16)
    convolved = long_convolution(signal, long_filter, skip_gain).astype(jnp.bfloat16)
    gated_t = (short_q.astype(jnp.float32) * convolved.astype(jnp.float32)).astype(jnp.bfloat16)
    outgoing = gated_t.reshape(per_group, groups, rows).transpose(1, 0, 2)
    both = jnp.broadcast_to(outgoing[None], (2,) + outgoing.shape).reshape((2 * groups,) + outgoing.shape[1:])
    returned = lax.all_to_all(both, ("yh",) + SEQ, split_axis=0, concat_axis=0, tiled=True)
    held = returned.reshape(2, width, rows).transpose(0, 2, 1)
    pieces, order = gather_pairs(held)
    weight = out_weight.reshape(-1, width, out_weight.shape[1])[order]
    result = jnp.einsum("pqtc,pqcj->tj", pieces, weight, preferred_element_type=jnp.float32)
    return result.astype(jnp.bfloat16)


SEQ = ("z", "ylo", "core")
CHAN = ("x", "yh")


def solution(mesh):
    shape = mesh.devices.shape
    fine = Mesh(mesh.devices.reshape(shape[0] // 8, 4, 2, shape[1] // 2, 2), SEQ + CHAN)
    in_specs = (
        P(SEQ, CHAN),
        P(SEQ, CHAN),
        P(SEQ, CHAN),
        P(None, None, CHAN),
        P(CHAN + SEQ, None),
        P(CHAN + SEQ),
        P(None, CHAN),
    )
    out_specs = P(SEQ, CHAN)
    return jax.shard_map(body, mesh=fine, in_specs=in_specs, out_specs=out_specs, check_vma=False)
```

```python
import math

import jax
import jax.numpy as jnp
from jax import lax
from jax.sharding import Mesh, PartitionSpec as P

DFT_PRECISION = lax.Precision.HIGH


def tables(count):
    index = jnp.arange(count, dtype=jnp.int32)
    phase = (index[:, None] * index[None, :] % count).astype(jnp.float32) * (2.0 * math.pi / count)
    return (jnp.cos(phase), jnp.sin(phase))


def twiddle(outer, inner, total):
    first = jnp.arange(outer, dtype=jnp.int32)
    second = jnp.arange(inner, dtype=jnp.int32)
    phase = (first[:, None] * second[None, :] % total).astype(jnp.float32) * (2.0 * math.pi / total)
    return (jnp.cos(phase), jnp.sin(phase))


def split_factor(length):
    total = 2 * length
    best = 1
    candidate = 1
    while candidate * candidate <= total:
        if length % candidate == 0:
            best = candidate
        candidate += 1
    return (best, total // best)


def rotation(cos_t, sin_t, sign):
    return jnp.concatenate(
        [jnp.concatenate([cos_t, sign * sin_t], 1), jnp.concatenate([-sign * sin_t, cos_t], 1)], 0
    )


def spectrum(signal, inner, outer, outer_tables, inner_tables, turn_tables):
    cos_out, sin_out = outer_tables
    cos_in, sin_in = inner_tables
    turn_cos, turn_sin = turn_tables
    used = signal.shape[1] // inner
    blocks = signal.reshape(signal.shape[0], used, inner)
    stacked = jnp.concatenate([cos_out[:, :used], -sin_out[:, :used]], 0)
    first = jnp.einsum("kn,cnm->ckm", stacked, blocks, precision=DFT_PRECISION)
    first_re, first_im = first[:, :outer], first[:, outer:]
    turned_re = first_re * turn_cos + first_im * turn_sin
    turned_im = first_im * turn_cos - first_re * turn_sin
    turned = jnp.concatenate([turned_re, turned_im], 2)
    second = jnp.einsum("ckm,mj->ckj", turned, rotation(cos_in, sin_in, -1.0), precision=DFT_PRECISION)
    return (second[..., :inner], second[..., inner:])


def long_convolution(mixed, filters, gains):
    channels, length = mixed.shape
    inner, outer = split_factor(length)
    total = 2 * length
    outer_tables = tables(outer)
    inner_tables = tables(inner)
    turn_tables = twiddle(outer, inner, total)
    signal = mixed.astype(jnp.float32)
    sig_re, sig_im = spectrum(signal, inner, outer, outer_tables, inner_tables, turn_tables)
    fil_re, fil_im = spectrum(filters, inner, outer, outer_tables, inner_tables, turn_tables)
    prod_re = sig_re * fil_re - sig_im * fil_im
    prod_im = sig_re * fil_im + sig_im * fil_re
    cos_in, sin_in = inner_tables
    product = jnp.concatenate([prod_re, prod_im], 2)
    back = jnp.einsum("ckj,jm->ckm", product, rotation(cos_in, sin_in, 1.0), precision=DFT_PRECISION)
    back_re, back_im = back[..., :inner], back[..., inner:]
    turn_cos, turn_sin = turn_tables
    rot_re = back_re * turn_cos - back_im * turn_sin
    rot_im = back_re * turn_sin + back_im * turn_cos
    cos_out, sin_out = outer_tables
    half = outer // 2
    stacked = jnp.concatenate([cos_out[:half], -sin_out[:half]], 1)
    result = jnp.einsum("nk,ckm->cnm", stacked, jnp.concatenate([rot_re, rot_im], 1), precision=DFT_PRECISION)
    return result.reshape(channels, length) / total + gains[:, None] * signal


def gather_pairs(held):
    size = lax.axis_size("x")
    mine = lax.axis_index("x")
    slots = [held]
    places = [mine]
    right = held
    left = held
    for step in range(1, size // 2 + 1):
        right = lax.ppermute(right, "x", [(i, (i + 1) % size) for i in range(size)])
        slots.append(right)
        places.append((mine - step) % size)
        if step < size - step:
            left = lax.ppermute(left, "x", [(i, (i - 1) % size) for i in range(size)])
            slots.append(left)
            places.append((mine + step) % size)
    place = jnp.stack(places)
    order = jnp.stack([place * 2, place * 2 + 1], axis=1)
    return jnp.stack(slots), order


def causal_filter(signal, taps):
    length = signal.shape[-1]
    total = taps[0][:, None] * signal
    for offset in range(1, taps.shape[0]):
        moved = jnp.concatenate(
            [jnp.zeros(signal.shape[:-1] + (offset,), signal.dtype), signal[..., : length - offset]], -1
        )
        total = total + taps[offset][:, None] * moved
    return total


def body(queries, keys, values, short_taps, long_filter, skip_gain, out_weight):
    rows, width = queries.shape
    groups = lax.axis_size(SEQ)
    per_group = width // groups
    seq_index = lax.axis_index(SEQ)
    raw = jnp.stack([queries.T, keys.T, values.T]).reshape(3, groups, per_group, rows).transpose(1, 0, 2, 3)
    split_raw = lax.all_to_all(raw, SEQ, split_axis=0, concat_axis=0, tiled=True)
    whole = split_raw.transpose(1, 2, 0, 3).reshape(3, per_group, groups * rows).astype(jnp.float32)
    own_taps = lax.dynamic_slice_in_dim(short_taps, seq_index * per_group, per_group, axis=2)
    short_q = causal_filter(whole[0], own_taps[0]).astype(jnp.bfloat16)
    signal = (causal_filter(whole[1], own_taps[1]) * causal_filter(whole[2], own_taps[2])).astype(jnp.bfloat16)
    convolved = long_convolution(signal, long_filter, skip_gain).astype(jnp.bfloat16)
    gated_t = (short_q.astype(jnp.float32) * convolved.astype(jnp.float32)).astype(jnp.bfloat16)
    outgoing = gated_t.reshape(per_group, groups, rows).transpose(1, 0, 2)
    both = jnp.broadcast_to(outgoing[None], (2,) + outgoing.shape).reshape((2 * groups,) + outgoing.shape[1:])
    returned = lax.all_to_all(both, ("yh",) + SEQ, split_axis=0, concat_axis=0, tiled=True)
    held = returned.reshape(2, width, rows).transpose(0, 2, 1)
    pieces, order = gather_pairs(held)
    weight = out_weight.reshape(-1, width, out_weight.shape[1])[order]
    result = jnp.einsum("pqtc,pqcj->tj", pieces, weight, preferred_element_type=jnp.float32)
    return result.astype(jnp.bfloat16)


SEQ = ("z", "ylo", "core")
CHAN = ("x", "yh")


def solution(mesh):
    shape = mesh.devices.shape
    fine = Mesh(mesh.devices.reshape(shape[0] // 8, 4, 2, shape[1] // 2, 2), SEQ + CHAN)
    in_specs = (
        P(SEQ, CHAN),
        P(SEQ, CHAN),
        P(SEQ, CHAN),
        P(None, None, CHAN),
        P(CHAN + SEQ, None),
        P(CHAN + SEQ),
        P(None, CHAN),
    )
    out_specs = P(SEQ, CHAN)
    return jax.shard_map(body, mesh=fine, in_specs=in_specs, out_specs=out_specs, check_vma=False)
```

```python
import math

import jax
import jax.numpy as jnp
from jax import lax
from jax.sharding import Mesh, PartitionSpec as P

DFT_PRECISION = lax.Precision.HIGH


def tables(count):
    index = jnp.arange(count, dtype=jnp.int32)
    phase = (index[:, None] * index[None, :] % count).astype(jnp.float32) * (2.0 * math.pi / count)
    return (jnp.cos(phase), jnp.sin(phase))


def twiddle(outer, inner, total):
    first = jnp.arange(outer, dtype=jnp.int32)
    second = jnp.arange(inner, dtype=jnp.int32)
    phase = (first[:, None] * second[None, :] % total).astype(jnp.float32) * (2.0 * math.pi / total)
    return (jnp.cos(phase), jnp.sin(phase))


def split_factor(length):
    total = 2 * length
    best = 1
    candidate = 1
    while candidate * candidate <= total:
        if length % candidate == 0:
            best = candidate
        candidate += 1
    return (best, total // best)


def rotation(cos_t, sin_t, sign):
    return jnp.concatenate(
        [jnp.concatenate([cos_t, sign * sin_t], 1), jnp.concatenate([-sign * sin_t, cos_t], 1)], 0
    )


def spectrum(signal, inner, outer, outer_tables, inner_tables, turn_tables):
    cos_out, sin_out = outer_tables
    cos_in, sin_in = inner_tables
    turn_cos, turn_sin = turn_tables
    used = signal.shape[1] // inner
    blocks = signal.reshape(signal.shape[0], used, inner)
    stacked = jnp.concatenate([cos_out[:, :used], -sin_out[:, :used]], 0)
    first = jnp.einsum("kn,cnm->ckm", stacked, blocks, precision=DFT_PRECISION)
    first_re, first_im = first[:, :outer], first[:, outer:]
    turned_re = first_re * turn_cos + first_im * turn_sin
    turned_im = first_im * turn_cos - first_re * turn_sin
    turned = jnp.concatenate([turned_re, turned_im], 2)
    second = jnp.einsum("ckm,mj->ckj", turned, rotation(cos_in, sin_in, -1.0), precision=DFT_PRECISION)
    return (second[..., :inner], second[..., inner:])


def long_convolution(mixed, filters, gains):
    channels, length = mixed.shape
    inner, outer = split_factor(length)
    total = 2 * length
    outer_tables = tables(outer)
    inner_tables = tables(inner)
    turn_tables = twiddle(outer, inner, total)
    signal = mixed.astype(jnp.float32)
    sig_re, sig_im = spectrum(signal, inner, outer, outer_tables, inner_tables, turn_tables)
    fil_re, fil_im = spectrum(filters, inner, outer, outer_tables, inner_tables, turn_tables)
    prod_re = sig_re * fil_re - sig_im * fil_im
    prod_im = sig_re * fil_im + sig_im * fil_re
    cos_in, sin_in = inner_tables
    product = jnp.concatenate([prod_re, prod_im], 2)
    back = jnp.einsum("ckj,jm->ckm", product, rotation(cos_in, sin_in, 1.0), precision=DFT_PRECISION)
    back_re, back_im = back[..., :inner], back[..., inner:]
    turn_cos, turn_sin = turn_tables
    rot_re = back_re * turn_cos - back_im * turn_sin
    rot_im = back_re * turn_sin + back_im * turn_cos
    cos_out, sin_out = outer_tables
    half = outer // 2
    stacked = jnp.concatenate([cos_out[:half], -sin_out[:half]], 1)
    result = jnp.einsum("nk,ckm->cnm", stacked, jnp.concatenate([rot_re, rot_im], 1), precision=DFT_PRECISION)
    return result.reshape(channels, length) / total + gains[:, None] * signal


def gather_pairs(held):
    size = lax.axis_size("x")
    mine = lax.axis_index("x")

    def moved(block, step):
        return lax.ppermute(block, "x", [(i, (i + step) % size) for i in range(size)])

    across = moved(held, size // 2)
    slots = [held, across]
    places = [mine, (mine + size // 2) % size]
    right = held
    left = held
    for step in range(1, size // 2):
        right = moved(right, 1)
        left = moved(left, -1)
        slots += [right, left]
        places += [(mine - step) % size, (mine + step) % size]
    place = jnp.stack(places)
    order = jnp.stack([place * 2, place * 2 + 1], axis=1)
    return jnp.stack(slots), order


def causal_filter(signal, taps):
    length = signal.shape[-1]
    total = taps[0][:, None] * signal
    for offset in range(1, taps.shape[0]):
        moved = jnp.concatenate(
            [jnp.zeros(signal.shape[:-1] + (offset,), signal.dtype), signal[..., : length - offset]], -1
        )
        total = total + taps[offset][:, None] * moved
    return total


def body(queries, keys, values, short_taps, long_filter, skip_gain, out_weight):
    rows, width = queries.shape
    groups = lax.axis_size(SEQ)
    per_group = width // groups
    seq_index = lax.axis_index(SEQ)
    raw = jnp.stack([queries.T, keys.T, values.T]).reshape(3, groups, per_group, rows).transpose(1, 0, 2, 3)
    split_raw = lax.all_to_all(raw, SEQ, split_axis=0, concat_axis=0, tiled=True)
    whole = split_raw.transpose(1, 2, 0, 3).reshape(3, per_group, groups * rows).astype(jnp.float32)
    own_taps = lax.dynamic_slice_in_dim(short_taps, seq_index * per_group, per_group, axis=2)
    short_q = causal_filter(whole[0], own_taps[0]).astype(jnp.bfloat16)
    signal = (causal_filter(whole[1], own_taps[1]) * causal_filter(whole[2], own_taps[2])).astype(jnp.bfloat16)
    convolved = long_convolution(signal, long_filter, skip_gain).astype(jnp.bfloat16)
    gated_t = (short_q.astype(jnp.float32) * convolved.astype(jnp.float32)).astype(jnp.bfloat16)
    outgoing = gated_t.reshape(per_group, groups, rows).transpose(1, 0, 2)
    both = jnp.broadcast_to(outgoing[None], (2,) + outgoing.shape).reshape((2 * groups,) + outgoing.shape[1:])
    returned = lax.all_to_all(both, ("yh",) + SEQ, split_axis=0, concat_axis=0, tiled=True)
    held = returned.reshape(2, width, rows).transpose(0, 2, 1)
    pieces, order = gather_pairs(held)
    weight = out_weight.reshape(-1, width, out_weight.shape[1])[order]
    result = jnp.einsum("pqtc,pqcj->tj", pieces, weight, preferred_element_type=jnp.float32)
    return result.astype(jnp.bfloat16)


SEQ = ("z", "ylo", "core")
CHAN = ("x", "yh")


def solution(mesh):
    shape = mesh.devices.shape
    fine = Mesh(mesh.devices.reshape(shape[0] // 8, 4, 2, shape[1] // 2, 2), SEQ + CHAN)
    in_specs = (
        P(SEQ, CHAN),
        P(SEQ, CHAN),
        P(SEQ, CHAN),
        P(None, None, CHAN),
        P(CHAN + SEQ, None),
        P(CHAN + SEQ),
        P(None, CHAN),
    )
    out_specs = P(SEQ, CHAN)
    return jax.shard_map(body, mesh=fine, in_specs=in_specs, out_specs=out_specs, check_vma=False)
```

```python
import math

import jax
import jax.numpy as jnp
from jax import lax
from jax.sharding import Mesh, PartitionSpec as P

DFT_PRECISION = lax.Precision.HIGH


def tables(count):
    index = jnp.arange(count, dtype=jnp.int32)
    phase = (index[:, None] * index[None, :] % count).astype(jnp.float32) * (2.0 * math.pi / count)
    return (jnp.cos(phase), jnp.sin(phase))


def twiddle(outer, inner, total):
    first = jnp.arange(outer, dtype=jnp.int32)
    second = jnp.arange(inner, dtype=jnp.int32)
    phase = (first[:, None] * second[None, :] % total).astype(jnp.float32) * (2.0 * math.pi / total)
    return (jnp.cos(phase), jnp.sin(phase))


def split_factor(length):
    total = 2 * length
    best = 1
    candidate = 1
    while candidate * candidate <= total:
        if length % candidate == 0:
            best = candidate
        candidate += 1
    return (best, total // best)


def rotation(cos_t, sin_t, sign):
    return jnp.concatenate(
        [jnp.concatenate([cos_t, sign * sin_t], 1), jnp.concatenate([-sign * sin_t, cos_t], 1)], 0
    )


def spectrum(signal, inner, outer, outer_tables, inner_tables, turn_tables):
    cos_out, sin_out = outer_tables
    cos_in, sin_in = inner_tables
    turn_cos, turn_sin = turn_tables
    used = signal.shape[1] // inner
    blocks = signal.reshape(signal.shape[0], used, inner)
    stacked = jnp.concatenate([cos_out[:, :used], -sin_out[:, :used]], 0)
    first = jnp.einsum("kn,cnm->ckm", stacked, blocks, precision=DFT_PRECISION)
    first_re, first_im = first[:, :outer], first[:, outer:]
    turned_re = first_re * turn_cos + first_im * turn_sin
    turned_im = first_im * turn_cos - first_re * turn_sin
    turned = jnp.concatenate([turned_re, turned_im], 2)
    second = jnp.einsum("ckm,mj->ckj", turned, rotation(cos_in, sin_in, -1.0), precision=DFT_PRECISION)
    return (second[..., :inner], second[..., inner:])


def long_convolution(mixed, filters, gains):
    channels, length = mixed.shape
    inner, outer = split_factor(length)
    total = 2 * length
    outer_tables = tables(outer)
    inner_tables = tables(inner)
    turn_tables = twiddle(outer, inner, total)
    signal = mixed.astype(jnp.float32)
    sig_re, sig_im = spectrum(signal, inner, outer, outer_tables, inner_tables, turn_tables)
    fil_re, fil_im = spectrum(filters, inner, outer, outer_tables, inner_tables, turn_tables)
    prod_re = sig_re * fil_re - sig_im * fil_im
    prod_im = sig_re * fil_im + sig_im * fil_re
    cos_in, sin_in = inner_tables
    product = jnp.concatenate([prod_re, prod_im], 2)
    back = jnp.einsum("ckj,jm->ckm", product, rotation(cos_in, sin_in, 1.0), precision=DFT_PRECISION)
    back_re, back_im = back[..., :inner], back[..., inner:]
    turn_cos, turn_sin = turn_tables
    rot_re = back_re * turn_cos - back_im * turn_sin
    rot_im = back_re * turn_sin + back_im * turn_cos
    cos_out, sin_out = outer_tables
    half = outer // 2
    stacked = jnp.concatenate([cos_out[:half], -sin_out[:half]], 1)
    result = jnp.einsum("nk,ckm->cnm", stacked, jnp.concatenate([rot_re, rot_im], 1), precision=DFT_PRECISION)
    return result.reshape(channels, length) / total + gains[:, None] * signal


def gather_pairs(held):
    size = lax.axis_size("x")
    mine = lax.axis_index("x")
    slots = [held]
    places = [mine]
    right = held
    left = held
    for step in range(1, size // 2 + 1):
        right = lax.ppermute(right, "x", [(i, (i + 1) % size) for i in range(size)])
        slots.append(right)
        places.append((mine - step) % size)
        if step < size - step:
            left = lax.ppermute(left, "x", [(i, (i - 1) % size) for i in range(size)])
            slots.append(left)
            places.append((mine + step) % size)
    place = jnp.stack(places)
    order = jnp.stack([place * 2, place * 2 + 1], axis=1)
    return jnp.stack(slots), order


def causal_filter(signal, taps):
    length = signal.shape[-1]
    total = taps[0][:, None] * signal
    for offset in range(1, taps.shape[0]):
        moved = jnp.concatenate(
            [jnp.zeros(signal.shape[:-1] + (offset,), signal.dtype), signal[..., : length - offset]], -1
        )
        total = total + taps[offset][:, None] * moved
    return total


def body(queries, keys, values, short_taps, long_filter, skip_gain, out_weight):
    rows, width = queries.shape
    groups = lax.axis_size(SEQ)
    per_group = width // groups
    seq_index = lax.axis_index(SEQ)
    raw = jnp.stack([queries.T, keys.T, values.T]).reshape(3, groups, per_group, rows).transpose(1, 0, 2, 3)
    split_raw = lax.all_to_all(raw, SEQ, split_axis=0, concat_axis=0, tiled=True)
    whole = split_raw.transpose(1, 2, 0, 3).reshape(3, per_group, groups * rows).astype(jnp.float32)
    own_taps = lax.dynamic_slice_in_dim(short_taps, seq_index * per_group, per_group, axis=2)
    short_q = causal_filter(whole[0], own_taps[0]).astype(jnp.bfloat16)
    signal = (causal_filter(whole[1], own_taps[1]) * causal_filter(whole[2], own_taps[2])).astype(jnp.bfloat16)
    convolved = long_convolution(signal, long_filter, skip_gain).astype(jnp.bfloat16)
    product = short_q.astype(jnp.float32) * convolved.astype(jnp.float32)
    gated_t = jnp.broadcast_to(product[None], (2,) + product.shape).astype(jnp.bfloat16)
    both = gated_t.reshape(2, per_group, groups, rows).transpose(0, 2, 1, 3).reshape(2 * groups, per_group, rows)
    returned = lax.all_to_all(both, ("yh",) + SEQ, split_axis=0, concat_axis=0, tiled=True)
    held = returned.reshape(2, width, rows).transpose(0, 2, 1)
    pieces, order = gather_pairs(held)
    weight = out_weight.reshape(-1, width, out_weight.shape[1])[order]
    result = sum(
        jnp.einsum("qtc,qcj->tj", pieces[p], weight[p], preferred_element_type=jnp.float32)
        for p in range(pieces.shape[0])
    )
    return result.astype(jnp.bfloat16)


SEQ = ("z", "ylo", "core")
CHAN = ("x", "yh")


def solution(mesh):
    shape = mesh.devices.shape
    fine = Mesh(mesh.devices.reshape(shape[0] // 8, 4, 2, shape[1] // 2, 2), SEQ + CHAN)
    in_specs = (
        P(SEQ, CHAN),
        P(SEQ, CHAN),
        P(SEQ, CHAN),
        P(None, None, CHAN),
        P(CHAN + SEQ, None),
        P(CHAN + SEQ),
        P(None, CHAN),
    )
    out_specs = P(SEQ, CHAN)
    return jax.shard_map(body, mesh=fine, in_specs=in_specs, out_specs=out_specs, check_vma=False)
```

```python
import math

import jax
import jax.numpy as jnp
from jax import lax
from jax.sharding import Mesh, PartitionSpec as P

DFT_PRECISION = lax.Precision.HIGH


def tables(count):
    index = jnp.arange(count, dtype=jnp.int32)
    phase = (index[:, None] * index[None, :] % count).astype(jnp.float32) * (2.0 * math.pi / count)
    return (jnp.cos(phase), jnp.sin(phase))


def twiddle(outer, inner, total):
    first = jnp.arange(outer, dtype=jnp.int32)
    second = jnp.arange(inner, dtype=jnp.int32)
    phase = (first[:, None] * second[None, :] % total).astype(jnp.float32) * (2.0 * math.pi / total)
    return (jnp.cos(phase), jnp.sin(phase))


def split_factor(length):
    total = 2 * length
    best = 1
    candidate = 1
    while candidate * candidate <= total:
        if length % candidate == 0:
            best = candidate
        candidate += 1
    return (best, total // best)


def rotation(cos_t, sin_t, sign):
    return jnp.concatenate(
        [jnp.concatenate([cos_t, sign * sin_t], 1), jnp.concatenate([-sign * sin_t, cos_t], 1)], 0
    )


def spectrum(signal, inner, outer, outer_tables, inner_tables, turn_tables):
    cos_out, sin_out = outer_tables
    cos_in, sin_in = inner_tables
    turn_cos, turn_sin = turn_tables
    used = signal.shape[1] // inner
    blocks = signal.reshape(signal.shape[0], used, inner)
    stacked = jnp.concatenate([cos_out[:, :used], -sin_out[:, :used]], 0)
    first = jnp.einsum("kn,cnm->ckm", stacked, blocks, precision=DFT_PRECISION)
    first_re, first_im = first[:, :outer], first[:, outer:]
    turned_re = first_re * turn_cos + first_im * turn_sin
    turned_im = first_im * turn_cos - first_re * turn_sin
    turned = jnp.concatenate([turned_re, turned_im], 2)
    second = jnp.einsum("ckm,mj->ckj", turned, rotation(cos_in, sin_in, -1.0), precision=DFT_PRECISION)
    return (second[..., :inner], second[..., inner:])


def long_convolution(mixed, filters, gains):
    channels, length = mixed.shape
    inner, outer = split_factor(length)
    total = 2 * length
    outer_tables = tables(outer)
    inner_tables = tables(inner)
    turn_tables = twiddle(outer, inner, total)
    signal = mixed.astype(jnp.float32)
    sig_re, sig_im = spectrum(signal, inner, outer, outer_tables, inner_tables, turn_tables)
    fil_re, fil_im = spectrum(filters, inner, outer, outer_tables, inner_tables, turn_tables)
    prod_re = sig_re * fil_re - sig_im * fil_im
    prod_im = sig_re * fil_im + sig_im * fil_re
    cos_in, sin_in = inner_tables
    product = jnp.concatenate([prod_re, prod_im], 2)
    back = jnp.einsum("ckj,jm->ckm", product, rotation(cos_in, sin_in, 1.0), precision=DFT_PRECISION)
    back_re, back_im = back[..., :inner], back[..., inner:]
    turn_cos, turn_sin = turn_tables
    rot_re = back_re * turn_cos - back_im * turn_sin
    rot_im = back_re * turn_sin + back_im * turn_cos
    cos_out, sin_out = outer_tables
    half = outer // 2
    stacked = jnp.concatenate([cos_out[:half], -sin_out[:half]], 1)
    result = jnp.einsum("nk,ckm->cnm", stacked, jnp.concatenate([rot_re, rot_im], 1), precision=DFT_PRECISION)
    return result.reshape(channels, length) / total + gains[:, None] * signal


def gather_pairs(held):
    size = lax.axis_size("x")
    mine = lax.axis_index("x")
    slots = [held]
    places = [mine]
    right = held
    left = held
    for step in range(1, size // 2 + 1):
        right = lax.ppermute(right, "x", [(i, (i + 1) % size) for i in range(size)])
        slots.append(right)
        places.append((mine - step) % size)
        if step < size - step:
            left = lax.ppermute(left, "x", [(i, (i - 1) % size) for i in range(size)])
            slots.append(left)
            places.append((mine + step) % size)
    place = jnp.stack(places)
    order = jnp.stack([place * 2, place * 2 + 1], axis=1)
    return jnp.stack(slots), order


def causal_filter(signal, taps):
    length = signal.shape[-1]
    total = taps[0][:, None] * signal
    for offset in range(1, taps.shape[0]):
        moved = jnp.concatenate(
            [jnp.zeros(signal.shape[:-1] + (offset,), signal.dtype), signal[..., : length - offset]], -1
        )
        total = total + taps[offset][:, None] * moved
    return total


def body(queries, keys, values, short_taps, long_filter, skip_gain, out_weight):
    rows, width = queries.shape
    groups = lax.axis_size(SEQ)
    per_group = width // groups
    seq_index = lax.axis_index(SEQ)
    raw = jnp.stack([queries.T, keys.T, values.T]).reshape(3, groups, per_group, rows).transpose(1, 0, 2, 3)
    split_raw = lax.all_to_all(raw, SEQ, split_axis=0, concat_axis=0, tiled=True)
    whole = split_raw.transpose(1, 2, 0, 3).reshape(3, per_group, groups * rows).astype(jnp.float32)
    own_taps = lax.dynamic_slice_in_dim(short_taps, seq_index * per_group, per_group, axis=2)
    short_q = causal_filter(whole[0], own_taps[0]).astype(jnp.bfloat16)
    signal = (causal_filter(whole[1], own_taps[1]) * causal_filter(whole[2], own_taps[2])).astype(jnp.bfloat16)
    convolved = long_convolution(signal, long_filter, skip_gain).astype(jnp.bfloat16)
    gated_t = (short_q.astype(jnp.float32) * convolved.astype(jnp.float32)).astype(jnp.bfloat16)
    outgoing = gated_t.reshape(per_group, groups, rows).transpose(1, 0, 2)
    both = jnp.concatenate([outgoing, outgoing], 0)
    returned = lax.all_to_all(both, ("yh",) + SEQ, split_axis=0, concat_axis=0, tiled=True)
    held = returned.reshape(2, width, rows).transpose(0, 2, 1)
    pieces, order = gather_pairs(held)
    weight = out_weight.reshape(-1, width, out_weight.shape[1])[order]
    result = jnp.einsum("pqtc,pqcj->tj", pieces, weight, preferred_element_type=jnp.float32)
    return result.astype(jnp.bfloat16)


SEQ = ("z", "ylo", "core")
CHAN = ("x", "yh")


def solution(mesh):
    shape = mesh.devices.shape
    fine = Mesh(mesh.devices.reshape(shape[0] // 8, 4, 2, shape[1] // 2, 2), SEQ + CHAN)
    in_specs = (
        P(SEQ, CHAN),
        P(SEQ, CHAN),
        P(SEQ, CHAN),
        P(None, None, CHAN),
        P(CHAN + SEQ, None),
        P(CHAN + SEQ),
        P(None, CHAN),
    )
    out_specs = P(SEQ, CHAN)
    return jax.shard_map(body, mesh=fine, in_specs=in_specs, out_specs=out_specs, check_vma=False)
```

```python
import math

import jax
import jax.numpy as jnp
from jax import lax
from jax.sharding import Mesh, PartitionSpec as P

DFT_PRECISION = lax.Precision.HIGH


def tables(count):
    index = jnp.arange(count, dtype=jnp.int32)
    phase = (index[:, None] * index[None, :] % count).astype(jnp.float32) * (2.0 * math.pi / count)
    return (jnp.cos(phase), jnp.sin(phase))


def twiddle(outer, inner, total):
    first = jnp.arange(outer, dtype=jnp.int32)
    second = jnp.arange(inner, dtype=jnp.int32)
    phase = (first[:, None] * second[None, :] % total).astype(jnp.float32) * (2.0 * math.pi / total)
    return (jnp.cos(phase), jnp.sin(phase))


def split_factor(length):
    total = 2 * length
    best = 1
    candidate = 1
    while candidate * candidate <= total:
        if length % candidate == 0:
            best = candidate
        candidate += 1
    return (best, total // best)


def rotation(cos_t, sin_t, sign):
    return jnp.concatenate(
        [jnp.concatenate([cos_t, sign * sin_t], 1), jnp.concatenate([-sign * sin_t, cos_t], 1)], 0
    )


def spectrum(signal, inner, outer, outer_tables, inner_tables, turn_tables):
    cos_out, sin_out = outer_tables
    cos_in, sin_in = inner_tables
    turn_cos, turn_sin = turn_tables
    used = signal.shape[1] // inner
    blocks = signal.reshape(signal.shape[0], used, inner)
    stacked = jnp.concatenate([cos_out[:, :used], -sin_out[:, :used]], 0)
    first = jnp.einsum("kn,cnm->ckm", stacked, blocks, precision=DFT_PRECISION)
    first_re, first_im = first[:, :outer], first[:, outer:]
    turned_re = first_re * turn_cos + first_im * turn_sin
    turned_im = first_im * turn_cos - first_re * turn_sin
    turned = jnp.concatenate([turned_re, turned_im], 2)
    second = jnp.einsum("ckm,mj->ckj", turned, rotation(cos_in, sin_in, -1.0), precision=DFT_PRECISION)
    return (second[..., :inner], second[..., inner:])


def long_convolution(mixed, filters, gains):
    channels, length = mixed.shape
    inner, outer = split_factor(length)
    total = 2 * length
    outer_tables = tables(outer)
    inner_tables = tables(inner)
    turn_tables = twiddle(outer, inner, total)
    signal = mixed.astype(jnp.float32)
    sig_re, sig_im = spectrum(signal, inner, outer, outer_tables, inner_tables, turn_tables)
    fil_re, fil_im = spectrum(filters, inner, outer, outer_tables, inner_tables, turn_tables)
    prod_re = sig_re * fil_re - sig_im * fil_im
    prod_im = sig_re * fil_im + sig_im * fil_re
    cos_in, sin_in = inner_tables
    product = jnp.concatenate([prod_re, prod_im], 2)
    back = jnp.einsum("ckj,jm->ckm", product, rotation(cos_in, sin_in, 1.0), precision=DFT_PRECISION)
    back_re, back_im = back[..., :inner], back[..., inner:]
    turn_cos, turn_sin = turn_tables
    rot_re = back_re * turn_cos - back_im * turn_sin
    rot_im = back_re * turn_sin + back_im * turn_cos
    cos_out, sin_out = outer_tables
    half = outer // 2
    stacked = jnp.concatenate([cos_out[:half], -sin_out[:half]], 1)
    result = jnp.einsum("nk,ckm->cnm", stacked, jnp.concatenate([rot_re, rot_im], 1), precision=DFT_PRECISION)
    return result.reshape(channels, length) / total + gains[:, None] * signal


def gather_pairs(held):
    size = lax.axis_size("x")
    mine = lax.axis_index("x")
    slots = [held]
    places = [mine]
    right = held
    left = held
    for step in range(1, size // 2 + 1):
        right = lax.ppermute(right, "x", [(i, (i + 1) % size) for i in range(size)])
        slots.append(right)
        places.append((mine - step) % size)
        if step < size - step:
            left = lax.ppermute(left, "x", [(i, (i - 1) % size) for i in range(size)])
            slots.append(left)
            places.append((mine + step) % size)
    place = jnp.stack(places)
    order = jnp.stack([place * 2, place * 2 + 1], axis=1)
    return jnp.stack(slots), order


def causal_filter(signal, taps):
    length = signal.shape[-1]
    total = taps[0][:, None] * signal
    for offset in range(1, taps.shape[0]):
        moved = jnp.concatenate(
            [jnp.zeros(signal.shape[:-1] + (offset,), signal.dtype), signal[..., : length - offset]], -1
        )
        total = total + taps[offset][:, None] * moved
    return total


def body(queries, keys, values, short_taps, long_filter, skip_gain, out_weight):
    rows, width = queries.shape
    groups = lax.axis_size(SEQ)
    per_group = width // groups
    seq_index = lax.axis_index(SEQ)
    raw = jnp.stack([queries.T, keys.T, values.T]).reshape(3, groups, per_group, rows).transpose(1, 0, 2, 3)
    split_raw = lax.all_to_all(raw, SEQ, split_axis=0, concat_axis=0, tiled=True)
    whole = split_raw.transpose(1, 2, 0, 3).reshape(3, per_group, groups * rows).astype(jnp.float32)
    own_taps = lax.dynamic_slice_in_dim(short_taps, seq_index * per_group, per_group, axis=2)
    short_q = causal_filter(whole[0], own_taps[0]).astype(jnp.bfloat16)
    signal = (causal_filter(whole[1], own_taps[1]) * causal_filter(whole[2], own_taps[2])).astype(jnp.bfloat16)
    convolved = long_convolution(signal, long_filter, skip_gain).astype(jnp.bfloat16)
    gated_t = (short_q.astype(jnp.float32) * convolved.astype(jnp.float32)).astype(jnp.bfloat16)
    outgoing = gated_t.reshape(per_group, groups, rows).transpose(1, 0, 2)
    both = jnp.concatenate([outgoing, outgoing], 0)
    returned = lax.all_to_all(both, ("yh",) + SEQ, split_axis=0, concat_axis=0, tiled=True)
    held = returned.reshape(2, width, rows).transpose(0, 2, 1)
    pieces, order = gather_pairs(held)
    weight = out_weight.reshape(-1, width, out_weight.shape[1])[order]
    early = jnp.einsum("pqtc,pqcj->tj", pieces[:-1], weight[:-1], preferred_element_type=jnp.float32)
    result = early + jnp.einsum("qtc,qcj->tj", pieces[-1], weight[-1], preferred_element_type=jnp.float32)
    return result.astype(jnp.bfloat16)


SEQ = ("z", "ylo", "core")
CHAN = ("x", "yh")


def solution(mesh):
    shape = mesh.devices.shape
    fine = Mesh(mesh.devices.reshape(shape[0] // 8, 4, 2, shape[1] // 2, 2), SEQ + CHAN)
    in_specs = (
        P(SEQ, CHAN),
        P(SEQ, CHAN),
        P(SEQ, CHAN),
        P(None, None, CHAN),
        P(CHAN + SEQ, None),
        P(CHAN + SEQ),
        P(None, CHAN),
    )
    out_specs = P(SEQ, CHAN)
    return jax.shard_map(body, mesh=fine, in_specs=in_specs, out_specs=out_specs, check_vma=False)
```
